256 devices in a mesh: row: 16 (over y_lo, x, core), col: 16 (over y_hi, z).
Axes of the slice: x: 4, y: 4 (y_hi: 2, y_lo: 2; y = y_hi * 2 + y_lo), z: 8, core: 2. Of those that a mesh axis runs over, the one named last changes fastest.
Arguments:
- tiles: bfloat16 [16, 16, 128, 128, 128], P('row', 'col'), as said below
- coords: int32 [16, 16, 2, 128], P('row', 'col'), may hold values from 0 to 63, as said below
- counts: int32 [16, 16], P('row', 'col'), may hold values from 1 to 128, as said below
- valid: int32 [131072], P(('row', 'col')), may hold values 0 or 1
- start: float32 [8, 131072], P(None, ('row', 'col'))
- rotations: float32 [2, 8, 24], replicated, as said below
Outputs:
- eigenmaps: float32 [8, 131072], P(None, ('row', 'col'))
- ritz: float32 [8, 8], replicated
The draws below stay inside these ranges and needn't reach their ends.
Inputs may be any that keep to these rules, and one draw needn't show every extreme that they name: coords[r, c, 0, s] is a block row from 0 to 63 and coords[r, c, 1, s] a block column from 0 to 63; the live slots of one owner name distinct blocks, each on or above the block diagonal (g_row <= g_col). The live slots of an owner are the first counts[r, c] of its list; one owner in grid row 0 has all 128 live. `tiles`: nonnegative; a tile on the block diagonal is symmetric. The Rayleigh-Ritz coefficients of the current vectors, rotations[t, :, 0 to 7], form a matrix whose diagonal dominates its rows.
All inputs are finite; a program needn't handle non-finite values. No bound on the sum of `valid` on one device may be relied on, other than what follows from the above.
Results may differ from the reference program's by a relative error of at most 0.0013.
Values may be sent and summed in bfloat16 or wider, within the bound.
No kernel may reach another device: no remote copies, remote signals or barrier semaphores. Data moves between devices by JAX's collectives and lax.ppermute only.
A program may use at most 64 MiB of HBM per device.

```python
import math
import jax
import jax.numpy as jnp
from jax import lax

TILE = 128
VECS = 8
ITERS = 2
STRETCH = 512
SLOTS = 128
NODES = 131072
BLOCKS = 1024
N_ROW = 16
N_COL = 16


def owner_layout(key):
    per_stretch = STRETCH // TILE
    row_span = N_COL * per_stretch
    col_span = N_ROW * per_stretch
    cells = row_span * col_span
    cell_index = jnp.arange(cells, dtype=jnp.int32)
    block_rows = cell_index // col_span
    block_cols = cell_index % col_span
    row_owner = jnp.arange(N_ROW, dtype=jnp.int32)[:, None, None]
    col_owner = jnp.arange(N_COL, dtype=jnp.int32)[None, :, None]
    global_rows = row_owner * row_span + block_rows[None, None, :]
    global_cols = (block_cols[None, None, :] // per_stretch * N_COL + col_owner) * per_stretch + block_cols[None, None, :] % per_stretch
    upper = global_rows <= global_cols
    spread = 2 ** 30 // cells
    noise = jax.random.randint(jax.random.fold_in(key, 1), (N_ROW, N_COL, cells), 0, spread, dtype=jnp.int32)
    score = noise * cells + cell_index[None, None, :] + jnp.where(upper, 0, 2 ** 30).astype(jnp.int32)
    score = jnp.where(cell_index[None, None, :] == col_span - 1, -1, score).astype(jnp.int32)
    chosen = jnp.argsort(score, axis=-1, stable=True)[..., :SLOTS].astype(jnp.int32)
    coords = jnp.stack([chosen // col_span, chosen % col_span], axis=2).astype(jnp.int32)
    available = jnp.sum(upper.astype(jnp.int32), axis=-1)
    divisor = 1 + jax.random.randint(jax.random.fold_in(key, 2), (N_ROW, N_COL), 0, 5, dtype=jnp.int32)
    wanted = jnp.maximum(1, SLOTS // divisor)
    full_col = jax.random.randint(jax.random.fold_in(key, 3), (), 0, N_COL, dtype=jnp.int32)
    is_full = (jnp.arange(N_ROW, dtype=jnp.int32)[:, None] == 0) & (jnp.arange(N_COL, dtype=jnp.int32)[None, :] == full_col)
    wanted = jnp.where(is_full, SLOTS, wanted)
    counts = jnp.minimum(wanted, available).astype(jnp.int32)
    return (coords, counts)


def draw_coords(key, part):
    return owner_layout(jax.random.fold_in(key, 7))[0]


def draw_counts(key, part):
    return owner_layout(jax.random.fold_in(key, 7))[1]


def draw_tiles(key, part):
    coords, counts = owner_layout(jax.random.fold_in(key, 7))
    per_stretch = STRETCH // TILE
    row_span = N_COL * per_stretch
    row_owner = jnp.arange(N_ROW, dtype=jnp.int32)[:, None, None]
    col_owner = jnp.arange(N_COL, dtype=jnp.int32)[None, :, None]
    global_rows = row_owner * row_span + coords[:, :, 0, :]
    global_cols = (coords[:, :, 1, :] // per_stretch * N_COL + col_owner) * per_stretch + coords[:, :, 1, :] % per_stretch
    on_diagonal = global_rows == global_cols
    shape = (N_ROW, N_COL, SLOTS, TILE, TILE)
    total_live = jnp.sum(counts).astype(jnp.float32)
    tiles_per_block = 2.0 * total_live / BLOCKS
    keep_share = jnp.minimum(1.0, 16.0 / (TILE * tiles_per_block))
    keep = jax.random.uniform(jax.random.fold_in(key, 12), shape, jnp.float32) < keep_share
    base = jnp.exp(-3.0 * jax.random.uniform(jax.random.fold_in(key, 11), shape, jnp.float32))
    weights = jnp.where(keep, base, 0.0) * 0.125
    mirrored = 0.5 * (weights + jnp.swapaxes(weights, -1, -2))
    weights = jnp.where(on_diagonal[..., None, None], mirrored, weights)
    return weights.astype(jnp.bfloat16)


def draw_start(key, part):
    positions = jnp.arange(NODES, dtype=jnp.float32) / NODES
    rising = jnp.exp(math.log(3.0) * positions)[None, :]
    values = jax.random.normal(jax.random.fold_in(key, 21), (VECS, NODES), jnp.float32)
    return (values * rising).astype(jnp.float32)


def draw_rotations(key, part):
    shape = (ITERS, VECS, 3 * VECS)
    row_at = jnp.arange(VECS, dtype=jnp.int32)[None, :, None]
    col_at = jnp.arange(3 * VECS, dtype=jnp.int32)[None, None, :]
    spread = jax.random.uniform(jax.random.fold_in(key, 31), shape, jnp.float32, -1.0, 1.0)
    normal_part = jax.random.normal(jax.random.fold_in(key, 32), shape, jnp.float32)
    leading = jnp.where(row_at == col_at, 1.0, 0.12 * spread)
    return jnp.where(col_at < VECS, leading, 0.5 * normal_part).astype(jnp.float32)


def set_ends(values, rng, low, high):
    longest = values.shape.index(max(values.shape))
    spots = []
    for shift in (0, 1):
        where = [jax.random.randint(jax.random.fold_in(rng, axis), (), 0, length) for axis, length in enumerate(values.shape)]
        where[longest] = (where[longest] + shift) % values.shape[longest]
        spots.append(tuple(where))
    return values.at[spots[0]].set(low).at[spots[1]].set(high)


def setup_inputs(seed: int = 0) -> dict:
    key_list = jax.random.split(jax.random.key(seed), 7)
    return {
        "tiles": draw_tiles(jax.random.fold_in(key_list[6], 71), 0),
        "coords": draw_coords(jax.random.fold_in(key_list[6], 71), 0),
        "counts": draw_counts(jax.random.fold_in(key_list[6], 71), 0),
        "valid": set_ends((jax.random.randint(key_list[3], (NODES,), 0, 8) < 7).astype(jnp.int32), jax.random.fold_in(key_list[3], 1), 0, 1),
        "start": draw_start(jax.random.fold_in(key_list[6], 71), 0),
        "rotations": draw_rotations(jax.random.fold_in(key_list[6], 71), 0),
    }


def matmul_high(left, right):
    return jnp.dot(left, right, precision=lax.Precision.HIGHEST)

def lower_inverse(lower_factor):
    order_size = lower_factor.shape[0]
    identity = jnp.eye(order_size, dtype=lower_factor.dtype)
    inverse_rows = []
    for row_at in range(order_size):
        partial_row = identity[row_at]
        for prior_at in range(row_at):
            partial_row = partial_row - lower_factor[row_at, prior_at] * inverse_rows[prior_at]
        inverse_rows.append(partial_row / lower_factor[row_at, row_at])
    return jnp.stack(inverse_rows)

def settle(new_vecs, new_images, new_steps, step_images, gram_x, gram_ax):
    node_total = jnp.float32(NODES)
    lower_factor = jnp.linalg.cholesky(gram_x / node_total)
    inverse = lower_inverse(lower_factor)
    theta = matmul_high(matmul_high(inverse, gram_ax / node_total), inverse.T)
    return (matmul_high(inverse, new_vecs), matmul_high(inverse, new_images), matmul_high(inverse, new_steps), matmul_high(inverse, step_images), theta)

def graph_product(vectors, tiles, coords, counts):
    width = vectors.shape[0]
    per_stretch = STRETCH // TILE
    row_span = N_COL * per_stretch
    owners = N_ROW * N_COL
    blocks = vectors.reshape(width, BLOCKS, TILE)
    flat_tiles = tiles.reshape(owners, SLOTS, TILE, TILE)
    flat_coords = coords.reshape(owners, 2, SLOTS)
    flat_counts = counts.reshape(owners)

    def visit(total, inputs):
        owner_tiles, owner_coords, owner_count, owner_id = inputs
        row_owner = owner_id // N_COL
        col_owner = owner_id % N_COL
        block_rows = owner_coords[0]
        block_cols = owner_coords[1]
        global_rows = row_owner * row_span + block_rows
        global_cols = (block_cols // per_stretch * N_COL + col_owner) * per_stretch + block_cols % per_stretch
        live = (jnp.arange(SLOTS, dtype=jnp.int32) < owner_count).astype(jnp.float32)
        mirror_weight = live * (global_rows != global_cols).astype(jnp.float32)
        dense = owner_tiles.astype(jnp.float32)
        col_values = blocks[:, global_cols].astype(jnp.float32)
        row_values = blocks[:, global_rows].astype(jnp.float32)
        direct = jnp.einsum('sut,cst->csu', dense, col_values, precision=lax.Precision.HIGHEST) * live[None, :, None]
        mirror = jnp.einsum('sut,csu->cst', dense, row_values, precision=lax.Precision.HIGHEST) * mirror_weight[None, :, None]
        total = total.at[:, global_rows].add(direct).at[:, global_cols].add(mirror)
        return (total, None)
    start_total = jnp.zeros((width, BLOCKS, TILE), jnp.float32)
    total = lax.scan(visit, start_total, (flat_tiles, flat_coords, flat_counts, jnp.arange(owners, dtype=jnp.int32)))[0]
    return total.reshape(width, NODES)

def reference(tiles, coords, counts, valid, start, rotations):
    node_mask = valid.astype(jnp.float32)
    first_vecs = start * node_mask[None, :]
    probe = jnp.concatenate([node_mask[None, :], first_vecs], 0).astype(jnp.bfloat16)
    raw = graph_product(probe, tiles, coords, counts)
    degree = raw[0]
    first_images = node_mask[None, :] * (degree[None, :] * first_vecs - raw[1:])
    zero_steps = jnp.zeros_like(first_vecs)
    vecs, images, steps, step_images, theta = settle(first_vecs, first_images, zero_steps, zero_steps, matmul_high(first_vecs, first_vecs.T), matmul_high(first_images, first_vecs.T))
    for turn in range(ITERS):
        resid = images - matmul_high(theta, vecs)
        resid_images = node_mask[None, :] * (degree[None, :] * resid - graph_product(resid.astype(jnp.bfloat16), tiles, coords, counts))
        stacked = jnp.concatenate([vecs, resid, steps], 0)
        stacked_images = jnp.concatenate([images, resid_images, step_images], 0)
        rotation = rotations[turn]
        new_vecs = matmul_high(rotation, stacked)
        new_images = matmul_high(rotation, stacked_images)
        new_steps = matmul_high(rotation[:, VECS:], stacked[VECS:])
        new_step_images = matmul_high(rotation[:, VECS:], stacked_images[VECS:])
        vecs, images, steps, step_images, theta = settle(new_vecs, new_images, new_steps, new_step_images, matmul_high(new_vecs, new_vecs.T), matmul_high(new_images, new_vecs.T))
    return (vecs, theta)
```

```python
import jax
import jax.numpy as jnp
from jax import lax
from jax.sharding import PartitionSpec as P


def matmul_high(left, right):
    return jnp.dot(left, right, precision=lax.Precision.HIGHEST)


def lower_inverse(lower_factor):
    order_size = lower_factor.shape[0]
    identity = jnp.eye(order_size, dtype=lower_factor.dtype)
    inverse_rows = []
    for row_at in range(order_size):
        partial_row = identity[row_at]
        for prior_at in range(row_at):
            partial_row = partial_row - lower_factor[row_at, prior_at] * inverse_rows[prior_at]
        inverse_rows.append(partial_row / lower_factor[row_at, row_at])
    return jnp.stack(inverse_rows)


def settle(new_vecs, new_images, new_steps, step_images, gram_x, gram_ax, node_total):
    lower_factor = jnp.linalg.cholesky(gram_x / node_total)
    inverse = lower_inverse(lower_factor)
    theta = matmul_high(matmul_high(inverse, gram_ax / node_total), inverse.T)
    return (
        matmul_high(inverse, new_vecs),
        matmul_high(inverse, new_images),
        matmul_high(inverse, new_steps),
        matmul_high(inverse, step_images),
        theta,
    )


def gather_by_exchange(local, axis):
    count = lax.axis_size(axis)
    copies = jnp.broadcast_to(local[None], (count,) + local.shape)
    held = lax.all_to_all(copies, axis, 0, 0, tiled=True)
    return jnp.swapaxes(held, 0, 1).reshape(local.shape[0], count * local.shape[1])


def scatter_sum_by_exchange(total, axis):
    count = lax.axis_size(axis)
    width, length = total.shape
    chunks = jnp.swapaxes(total.reshape(width, count, length // count), 0, 1)
    held = lax.all_to_all(chunks, axis, 0, 0, tiled=True)
    return jnp.sum(held, axis=0)


def gram_sums(new_vecs, new_images):
    local = jnp.stack([matmul_high(new_vecs, new_vecs.T), matmul_high(new_images, new_vecs.T)])
    count = lax.axis_size("row") * lax.axis_size("col")
    copies = jnp.broadcast_to(local[None], (count,) + local.shape)
    held = lax.all_to_all(copies, ("row", "col"), 0, 0, tiled=True)
    total = jnp.sum(held, axis=0)
    return total[0], total[1]


def local_terms(
    part_tiles, part_rows, part_cols, weight_direct, weight_mirror, col_blocks, row_blocks
):
    row_span = row_blocks.shape[1]
    col_span = col_blocks.shape[1]
    col_values = jnp.take(col_blocks, part_cols, axis=1)
    row_values = jnp.take(row_blocks, part_rows, axis=1)
    direct = (
        jnp.einsum("sut,cst->csu", part_tiles, col_values, preferred_element_type=jnp.float32)
        * weight_direct[None, :, None]
    )
    mirror = (
        jnp.einsum("sut,csu->cst", part_tiles, row_values, preferred_element_type=jnp.float32)
        * weight_mirror[None, :, None]
    )
    pick_rows = (part_rows[:, None] == jnp.arange(row_span, dtype=jnp.int32)[None, :]).astype(
        jnp.float32
    )
    pick_cols = (part_cols[:, None] == jnp.arange(col_span, dtype=jnp.int32)[None, :]).astype(
        jnp.float32
    )
    rows_sum = jnp.einsum("sp,csu->cpu", pick_rows, direct, precision=lax.Precision.HIGHEST)
    cols_sum = jnp.einsum("sq,cst->cqt", pick_cols, mirror, precision=lax.Precision.HIGHEST)
    return (rows_sum, cols_sum)


def body(tiles, coords, counts, valid, start, rotations):
    row_count = lax.axis_size("row")
    col_count = lax.axis_size("col")
    row_index = lax.axis_index("row")
    col_index = lax.axis_index("col")
    slot_count = tiles.shape[2]
    tile_side = tiles.shape[3]
    stretch_nodes = valid.shape[0]
    per_stretch = stretch_nodes // tile_side
    row_span = col_count * per_stretch
    col_span = row_count * per_stretch
    node_total = jnp.float32(stretch_nodes * row_count * col_count)
    vec_count = start.shape[0]
    flat_tiles = tiles.reshape(slot_count, tile_side, tile_side)
    block_rows = coords[0, 0, 0]
    block_cols = coords[0, 0, 1]
    live_count = counts[0, 0]
    global_rows = row_index * row_span + block_rows
    global_cols = (
        block_cols // per_stretch * col_count + col_index
    ) * per_stretch + block_cols % per_stretch
    live = (jnp.arange(slot_count, dtype=jnp.int32) < live_count).astype(jnp.float32)
    mirror_weight = live * (global_rows != global_cols).astype(jnp.float32)

    def graph_product(vectors):
        width = vectors.shape[0]
        short = vectors.astype(jnp.bfloat16)
        col_side = gather_by_exchange(short, "row")
        row_side = gather_by_exchange(short, "col")
        col_blocks = col_side.reshape(width, col_span, tile_side)
        row_blocks = row_side.reshape(width, row_span, tile_side)
        rows_total, cols_total = local_terms(
            flat_tiles, block_rows, block_cols, live, mirror_weight, col_blocks, row_blocks
        )
        direct_part = scatter_sum_by_exchange(rows_total.reshape(width, row_span * tile_side), "col")
        mirror_part = scatter_sum_by_exchange(cols_total.reshape(width, col_span * tile_side), "row")
        return direct_part + mirror_part

    node_mask = valid.astype(jnp.float32)
    first_vecs = start * node_mask[None, :]
    raw = graph_product(jnp.concatenate([node_mask[None, :], first_vecs], 0))
    degree = raw[0]
    first_images = node_mask[None, :] * (degree[None, :] * first_vecs - raw[1:])
    zero_steps = jnp.zeros_like(first_vecs)
    gram_x, gram_ax = gram_sums(first_vecs, first_images)
    vecs, images, steps, step_images, theta = settle(
        first_vecs, first_images, zero_steps, zero_steps, gram_x, gram_ax, node_total
    )
    for turn in range(rotations.shape[0]):
        resid = images - matmul_high(theta, vecs)
        resid_images = node_mask[None, :] * (degree[None, :] * resid - graph_product(resid))
        stacked = jnp.concatenate([vecs, resid, steps], 0)
        stacked_images = jnp.concatenate([images, resid_images, step_images], 0)
        rotation = rotations[turn]
        new_vecs = matmul_high(rotation, stacked)
        new_images = matmul_high(rotation, stacked_images)
        gram_x, gram_ax = gram_sums(new_vecs, new_images)
        new_steps = matmul_high(rotation[:, vec_count:], stacked[vec_count:])
        new_step_images = matmul_high(rotation[:, vec_count:], stacked_images[vec_count:])
        vecs, images, steps, step_images, theta = settle(
            new_vecs, new_images, new_steps, new_step_images, gram_x, gram_ax, node_total
        )
    return (vecs, theta)


def solution(mesh):
    in_specs = (
        P("row", "col", None, None, None),
        P("row", "col", None, None),
        P("row", "col"),
        P(("row", "col")),
        P(None, ("row", "col")),
        P(),
    )
    out_specs = (P(None, ("row", "col")), P())
    return jax.shard_map(body, mesh=mesh, in_specs=in_specs, out_specs=out_specs, check_vma=False)
```

```python
import jax
import jax.numpy as jnp
from jax import lax
from jax.sharding import PartitionSpec as P


def matmul_high(left, right):
    return jnp.dot(left, right, precision=lax.Precision.HIGHEST)


def lower_inverse(lower_factor):
    order_size = lower_factor.shape[0]
    assert order_size <= 8
    identity = jnp.eye(order_size, dtype=lower_factor.dtype)
    diagonal = jnp.diagonal(lower_factor)
    strict = lower_factor / diagonal[:, None] - identity
    square = matmul_high(strict, strict)
    fourth = matmul_high(square, square)
    inverse = matmul_high(matmul_high(identity - strict, identity + square), identity + fourth)
    return inverse / diagonal[None, :]


def settle(new_vecs, new_images, new_steps, step_images, gram_x, gram_ax, node_total):
    lower_factor = jnp.linalg.cholesky(gram_x / node_total)
    inverse = lower_inverse(lower_factor)
    theta = matmul_high(matmul_high(inverse, gram_ax / node_total), inverse.T)
    return (
        matmul_high(inverse, new_vecs),
        matmul_high(inverse, new_images),
        matmul_high(inverse, new_steps),
        matmul_high(inverse, step_images),
        theta,
    )


def gather_by_exchange(local, axis):
    count = lax.axis_size(axis)
    copies = jnp.broadcast_to(local[None], (count,) + local.shape)
    held = lax.all_to_all(copies, axis, 0, 0, tiled=True)
    return jnp.swapaxes(held, 0, 1).reshape(local.shape[0], count * local.shape[1])


def scatter_sum_by_exchange(total, axis):
    count = lax.axis_size(axis)
    width, length = total.shape
    chunks = jnp.swapaxes(total.reshape(width, count, length // count), 0, 1)
    held = lax.all_to_all(chunks, axis, 0, 0, tiled=True)
    return jnp.sum(held, axis=0)


def gram_sums(new_vecs, new_images):
    local = jnp.stack([matmul_high(new_vecs, new_vecs.T), matmul_high(new_images, new_vecs.T)])
    count = lax.axis_size("row") * lax.axis_size("col")
    copies = jnp.broadcast_to(local[None], (count,) + local.shape)
    held = lax.all_to_all(copies, ("row", "col"), 0, 0, tiled=True)
    total = jnp.sum(held, axis=0)
    return total[0], total[1]


def local_terms(
    part_tiles, part_rows, part_cols, weight_direct, weight_mirror, col_blocks, row_blocks
):
    row_span = row_blocks.shape[1]
    col_span = col_blocks.shape[1]
    col_values = jnp.take(col_blocks, part_cols, axis=1)
    row_values = jnp.take(row_blocks, part_rows, axis=1)
    direct = (
        jnp.einsum("sut,cst->csu", part_tiles, col_values, preferred_element_type=jnp.float32)
        * weight_direct[None, :, None]
    )
    mirror = (
        jnp.einsum("sut,csu->cst", part_tiles, row_values, preferred_element_type=jnp.float32)
        * weight_mirror[None, :, None]
    )
    pick_rows = (part_rows[:, None] == jnp.arange(row_span, dtype=jnp.int32)[None, :]).astype(
        jnp.float32
    )
    pick_cols = (part_cols[:, None] == jnp.arange(col_span, dtype=jnp.int32)[None, :]).astype(
        jnp.float32
    )
    rows_sum = jnp.einsum("sp,csu->cpu", pick_rows, direct, precision=lax.Precision.HIGHEST)
    cols_sum = jnp.einsum("sq,cst->cqt", pick_cols, mirror, precision=lax.Precision.HIGHEST)
    return (rows_sum, cols_sum)


def body(tiles, coords, counts, valid, start, rotations):
    row_count = lax.axis_size("row")
    col_count = lax.axis_size("col")
    row_index = lax.axis_index("row")
    col_index = lax.axis_index("col")
    slot_count = tiles.shape[2]
    tile_side = tiles.shape[3]
    stretch_nodes = valid.shape[0]
    per_stretch = stretch_nodes // tile_side
    row_span = col_count * per_stretch
    col_span = row_count * per_stretch
    node_total = jnp.float32(stretch_nodes * row_count * col_count)
    vec_count = start.shape[0]
    flat_tiles = tiles.reshape(slot_count, tile_side, tile_side)
    block_rows = coords[0, 0, 0]
    block_cols = coords[0, 0, 1]
    live_count = counts[0, 0]
    global_rows = row_index * row_span + block_rows
    global_cols = (
        block_cols // per_stretch * col_count + col_index
    ) * per_stretch + block_cols % per_stretch
    live = (jnp.arange(slot_count, dtype=jnp.int32) < live_count).astype(jnp.float32)
    mirror_weight = live * (global_rows != global_cols).astype(jnp.float32)

    def graph_product(vectors):
        width = vectors.shape[0]
        short = vectors.astype(jnp.bfloat16)
        col_side = gather_by_exchange(short, "row")
        row_side = gather_by_exchange(short, "col")
        col_blocks = col_side.reshape(width, col_span, tile_side)
        row_blocks = row_side.reshape(width, row_span, tile_side)
        rows_total, cols_total = local_terms(
            flat_tiles, block_rows, block_cols, live, mirror_weight, col_blocks, row_blocks
        )
        direct_part = scatter_sum_by_exchange(rows_total.reshape(width, row_span * tile_side), "col")
        mirror_part = scatter_sum_by_exchange(cols_total.reshape(width, col_span * tile_side), "row")
        return direct_part + mirror_part

    node_mask = valid.astype(jnp.float32)
    first_vecs = start * node_mask[None, :]
    raw = graph_product(jnp.concatenate([node_mask[None, :], first_vecs], 0))
    degree = raw[0]
    first_images = node_mask[None, :] * (degree[None, :] * first_vecs - raw[1:])
    zero_steps = jnp.zeros_like(first_vecs)
    gram_x, gram_ax = gram_sums(first_vecs, first_images)
    vecs, images, steps, step_images, theta = settle(
        first_vecs, first_images, zero_steps, zero_steps, gram_x, gram_ax, node_total
    )
    for turn in range(rotations.shape[0]):
        resid = images - matmul_high(theta, vecs)
        resid_images = node_mask[None, :] * (degree[None, :] * resid - graph_product(resid))
        stacked = jnp.concatenate([vecs, resid, steps], 0)
        stacked_images = jnp.concatenate([images, resid_images, step_images], 0)
        rotation = rotations[turn]
        new_vecs = matmul_high(rotation, stacked)
        new_images = matmul_high(rotation, stacked_images)
        gram_x, gram_ax = gram_sums(new_vecs, new_images)
        new_steps = matmul_high(rotation[:, vec_count:], stacked[vec_count:])
        new_step_images = matmul_high(rotation[:, vec_count:], stacked_images[vec_count:])
        vecs, images, steps, step_images, theta = settle(
            new_vecs, new_images, new_steps, new_step_images, gram_x, gram_ax, node_total
        )
    return (vecs, theta)


def solution(mesh):
    in_specs = (
        P("row", "col", None, None, None),
        P("row", "col", None, None),
        P("row", "col"),
        P(("row", "col")),
        P(None, ("row", "col")),
        P(),
    )
    out_specs = (P(None, ("row", "col")), P())
    return jax.shard_map(body, mesh=mesh, in_specs=in_specs, out_specs=out_specs, check_vma=False)
```

```python
import jax
import jax.numpy as jnp
from jax import lax
from jax.sharding import PartitionSpec as P


def matmul_high(left, right):
    return jnp.dot(left, right, precision=lax.Precision.HIGHEST)


def lower_inverse(lower_factor):
    order_size = lower_factor.shape[0]
    assert order_size <= 8
    identity = jnp.eye(order_size, dtype=lower_factor.dtype)
    diagonal = jnp.diagonal(lower_factor)
    strict = lower_factor / diagonal[:, None] - identity
    square = matmul_high(strict, strict)
    fourth = matmul_high(square, square)
    inverse = matmul_high(matmul_high(identity - strict, identity + square), identity + fourth)
    return inverse / diagonal[None, :]


def settle(new_vecs, new_images, new_steps, step_images, gram_x, gram_ax, node_total):
    lower_factor = jnp.linalg.cholesky(gram_x / node_total)
    inverse = lower_inverse(lower_factor)
    theta = matmul_high(matmul_high(inverse, gram_ax / node_total), inverse.T)
    return (
        matmul_high(inverse, new_vecs),
        matmul_high(inverse, new_images),
        matmul_high(inverse, new_steps),
        matmul_high(inverse, step_images),
        theta,
    )


def gather_by_exchange(local, axis):
    count = lax.axis_size(axis)
    copies = jnp.broadcast_to(local[None], (count,) + local.shape)
    held = lax.all_to_all(copies, axis, 0, 0, tiled=True)
    return jnp.swapaxes(held, 0, 1).reshape(local.shape[0], count * local.shape[1])


def scatter_sum_by_exchange(chunks, axis):
    held = lax.all_to_all(chunks, axis, 0, 0, tiled=True)
    return jnp.sum(held, axis=0)


def gram_sums(new_vecs, new_images):
    order = new_vecs.shape[0]
    local = jnp.concatenate(
        [matmul_high(new_vecs, new_vecs.T).reshape(-1), matmul_high(new_images, new_vecs.T).reshape(-1)]
    )
    count = lax.axis_size("row") * lax.axis_size("col")
    copies = jnp.broadcast_to(local[None], (count,) + local.shape)
    held = lax.all_to_all(copies, ("row", "col"), 0, 0, tiled=True)
    total = jnp.sum(held, axis=0)
    return total[: order * order].reshape(order, order), total[order * order :].reshape(order, order)


def local_terms(
    part_tiles,
    part_rows,
    part_cols,
    weight_direct,
    weight_mirror,
    col_blocks,
    row_blocks,
    row_owners,
    col_owners,
):
    row_span = row_blocks.shape[1]
    col_span = col_blocks.shape[1]
    col_values = jnp.take(col_blocks, part_cols, axis=1)
    row_values = jnp.take(row_blocks, part_rows, axis=1)
    direct = (
        jnp.einsum("sut,cst->csu", part_tiles, col_values, preferred_element_type=jnp.float32)
        * weight_direct[None, :, None]
    )
    mirror = (
        jnp.einsum("sut,csu->cst", part_tiles, row_values, preferred_element_type=jnp.float32)
        * weight_mirror[None, :, None]
    )
    pick_rows = (part_rows[:, None] == jnp.arange(row_span, dtype=jnp.int32)[None, :]).astype(
        jnp.float32
    )
    pick_cols = (part_cols[:, None] == jnp.arange(col_span, dtype=jnp.int32)[None, :]).astype(
        jnp.float32
    )
    slots = pick_rows.shape[0]
    rows_sum = jnp.einsum(
        "sjb,csu->jcbu",
        pick_rows.reshape(slots, row_owners, row_span // row_owners),
        direct,
        precision=lax.Precision.HIGHEST,
    )
    cols_sum = jnp.einsum(
        "sjb,cst->jcbt",
        pick_cols.reshape(slots, col_owners, col_span // col_owners),
        mirror,
        precision=lax.Precision.HIGHEST,
    )
    width = direct.shape[0]
    return (
        rows_sum.reshape(row_owners, width, -1),
        cols_sum.reshape(col_owners, width, -1),
    )


def body(tiles, coords, counts, valid, start, rotations):
    row_count = lax.axis_size("row")
    col_count = lax.axis_size("col")
    row_index = lax.axis_index("row")
    col_index = lax.axis_index("col")
    slot_count = tiles.shape[2]
    tile_side = tiles.shape[3]
    stretch_nodes = valid.shape[0]
    per_stretch = stretch_nodes // tile_side
    row_span = col_count * per_stretch
    col_span = row_count * per_stretch
    node_total = jnp.float32(stretch_nodes * row_count * col_count)
    vec_count = start.shape[0]
    flat_tiles = tiles.reshape(slot_count, tile_side, tile_side)
    block_rows = coords[0, 0, 0]
    block_cols = coords[0, 0, 1]
    live_count = counts[0, 0]
    global_rows = row_index * row_span + block_rows
    global_cols = (
        block_cols // per_stretch * col_count + col_index
    ) * per_stretch + block_cols % per_stretch
    live = (jnp.arange(slot_count, dtype=jnp.int32) < live_count).astype(jnp.float32)
    mirror_weight = live * (global_rows != global_cols).astype(jnp.float32)

    def graph_product(vectors):
        width = vectors.shape[0]
        short = vectors.astype(jnp.bfloat16)
        col_side = gather_by_exchange(short, "row")
        row_side = gather_by_exchange(short, "col")
        col_blocks = col_side.reshape(width, col_span, tile_side)
        row_blocks = row_side.reshape(width, row_span, tile_side)
        rows_total, cols_total = local_terms(
            flat_tiles,
            block_rows,
            block_cols,
            live,
            mirror_weight,
            col_blocks,
            row_blocks,
            col_count,
            row_count,
        )
        direct_part = scatter_sum_by_exchange(rows_total, "col")
        mirror_part = scatter_sum_by_exchange(cols_total, "row")
        return direct_part + mirror_part

    node_mask = valid.astype(jnp.float32)
    first_vecs = start * node_mask[None, :]
    raw = graph_product(jnp.concatenate([node_mask[None, :], first_vecs], 0))
    degree = raw[0]
    first_images = node_mask[None, :] * (degree[None, :] * first_vecs - raw[1:])
    zero_steps = jnp.zeros_like(first_vecs)
    gram_x, gram_ax = gram_sums(first_vecs, first_images)
    vecs, images, steps, step_images, theta = settle(
        first_vecs, first_images, zero_steps, zero_steps, gram_x, gram_ax, node_total
    )
    for turn in range(rotations.shape[0]):
        resid = images - matmul_high(theta, vecs)
        resid_images = node_mask[None, :] * (degree[None, :] * resid - graph_product(resid))
        stacked = jnp.concatenate([vecs, resid, steps], 0)
        stacked_images = jnp.concatenate([images, resid_images, step_images], 0)
        rotation = rotations[turn]
        new_vecs = matmul_high(rotation, stacked)
        new_images = matmul_high(rotation, stacked_images)
        gram_x, gram_ax = gram_sums(new_vecs, new_images)
        new_steps = matmul_high(rotation[:, vec_count:], stacked[vec_count:])
        new_step_images = matmul_high(rotation[:, vec_count:], stacked_images[vec_count:])
        vecs, images, steps, step_images, theta = settle(
            new_vecs, new_images, new_steps, new_step_images, gram_x, gram_ax, node_total
        )
    return (vecs, theta)


def solution(mesh):
    in_specs = (
        P("row", "col", None, None, None),
        P("row", "col", None, None),
        P("row", "col"),
        P(("row", "col")),
        P(None, ("row", "col")),
        P(),
    )
    out_specs = (P(None, ("row", "col")), P())
    return jax.shard_map(body, mesh=mesh, in_specs=in_specs, out_specs=out_specs, check_vma=False)
```

```python
import jax
import jax.numpy as jnp
from jax import lax
from jax.sharding import PartitionSpec as P


def matmul_high(left, right):
    return jnp.dot(left, right, precision=lax.Precision.HIGHEST)


def lower_inverse(lower_factor):
    order_size = lower_factor.shape[0]
    assert order_size <= 8
    identity = jnp.eye(order_size, dtype=lower_factor.dtype)
    diagonal = jnp.diagonal(lower_factor)
    strict = lower_factor / diagonal[:, None] - identity
    square = matmul_high(strict, strict)
    fourth = matmul_high(square, square)
    inverse = matmul_high(matmul_high(identity - strict, identity + square), identity + fourth)
    return inverse / diagonal[None, :]


def settle(new_vecs, new_images, new_steps, step_images, gram_x, gram_ax, node_total):
    lower_factor = jnp.linalg.cholesky(gram_x / node_total)
    inverse = lower_inverse(lower_factor)
    theta = matmul_high(matmul_high(inverse, gram_ax / node_total), inverse.T)
    return (
        matmul_high(inverse, new_vecs),
        matmul_high(inverse, new_images),
        matmul_high(inverse, new_steps),
        matmul_high(inverse, step_images),
        theta,
    )


def gather_by_exchange(local, axis):
    count = lax.axis_size(axis)
    copies = jnp.broadcast_to(local[None], (count,) + local.shape)
    held = lax.all_to_all(copies, axis, 0, 0, tiled=True)
    return jnp.swapaxes(held, 0, 1).reshape(local.shape[0], count * local.shape[1])


def scatter_sum_by_exchange(chunks, axis):
    held = lax.all_to_all(chunks, axis, 0, 0, tiled=True)
    return jnp.sum(held, axis=0)


def gram_sums(new_vecs, new_images):
    order = new_vecs.shape[0]
    local = jnp.concatenate(
        [matmul_high(new_vecs, new_vecs.T).reshape(-1), matmul_high(new_images, new_vecs.T).reshape(-1)]
    )
    count = lax.axis_size("row") * lax.axis_size("col")
    copies = jnp.broadcast_to(local[None], (count,) + local.shape)
    held = lax.all_to_all(copies, ("row", "col"), 0, 0, tiled=True)
    total = jnp.sum(held, axis=0)
    return total[: order * order].reshape(order, order), total[order * order :].reshape(order, order)


def block_sums(pick, part_values, owners):
    slots, span = pick.shape
    sums = jnp.einsum(
        "sjb,csu->jcbu",
        pick.reshape(slots, owners, span // owners),
        part_values,
        precision=lax.Precision.HIGHEST,
    )
    return sums.reshape(owners, part_values.shape[0], -1)


def direct_terms(part_tiles, part_rows, part_cols, weight_direct, col_blocks, row_span, owners):
    col_values = jnp.take(col_blocks, part_cols, axis=1)
    direct = (
        jnp.einsum("sut,cst->csu", part_tiles, col_values, preferred_element_type=jnp.float32)
        * weight_direct[None, :, None]
    )
    pick_rows = (part_rows[:, None] == jnp.arange(row_span, dtype=jnp.int32)[None, :]).astype(
        jnp.float32
    )
    return block_sums(pick_rows, direct, owners)


def mirror_terms(part_tiles, part_rows, part_cols, weight_mirror, row_blocks, col_span, owners):
    row_values = jnp.take(row_blocks, part_rows, axis=1)
    mirror = (
        jnp.einsum("sut,csu->cst", part_tiles, row_values, preferred_element_type=jnp.float32)
        * weight_mirror[None, :, None]
    )
    pick_cols = (part_cols[:, None] == jnp.arange(col_span, dtype=jnp.int32)[None, :]).astype(
        jnp.float32
    )
    return block_sums(pick_cols, mirror, owners)


def body(tiles, coords, counts, valid, start, rotations):
    row_count = lax.axis_size("row")
    col_count = lax.axis_size("col")
    row_index = lax.axis_index("row")
    col_index = lax.axis_index("col")
    slot_count = tiles.shape[2]
    tile_side = tiles.shape[3]
    stretch_nodes = valid.shape[0]
    per_stretch = stretch_nodes // tile_side
    row_span = col_count * per_stretch
    col_span = row_count * per_stretch
    node_total = jnp.float32(stretch_nodes * row_count * col_count)
    vec_count = start.shape[0]
    flat_tiles = tiles.reshape(slot_count, tile_side, tile_side)
    block_rows = coords[0, 0, 0]
    block_cols = coords[0, 0, 1]
    live_count = counts[0, 0]
    global_rows = row_index * row_span + block_rows
    global_cols = (
        block_cols // per_stretch * col_count + col_index
    ) * per_stretch + block_cols % per_stretch
    live = (jnp.arange(slot_count, dtype=jnp.int32) < live_count).astype(jnp.float32)
    mirror_weight = live * (global_rows != global_cols).astype(jnp.float32)

    def graph_product(vectors):
        width = vectors.shape[0]
        short = vectors.astype(jnp.bfloat16)
        col_side = gather_by_exchange(short, "row")
        col_blocks = col_side.reshape(width, col_span, tile_side)
        rows_total = direct_terms(
            flat_tiles, block_rows, block_cols, live, col_blocks, row_span, col_count
        )
        row_side = gather_by_exchange(short, "col")
        rows_total, row_side = lax.optimization_barrier((rows_total, row_side))
        row_blocks = row_side.reshape(width, row_span, tile_side)
        cols_total = mirror_terms(
            flat_tiles, block_rows, block_cols, mirror_weight, row_blocks, col_span, row_count
        )
        direct_part = scatter_sum_by_exchange(rows_total, "col")
        direct_part, cols_total = lax.optimization_barrier((direct_part, cols_total))
        mirror_part = scatter_sum_by_exchange(cols_total, "row")
        return direct_part + mirror_part

    node_mask = valid.astype(jnp.float32)
    first_vecs = start * node_mask[None, :]
    raw = graph_product(jnp.concatenate([node_mask[None, :], first_vecs], 0))
    degree = raw[0]
    first_images = node_mask[None, :] * (degree[None, :] * first_vecs - raw[1:])
    zero_steps = jnp.zeros_like(first_vecs)
    gram_x, gram_ax = gram_sums(first_vecs, first_images)
    vecs, images, steps, step_images, theta = settle(
        first_vecs, first_images, zero_steps, zero_steps, gram_x, gram_ax, node_total
    )
    for turn in range(rotations.shape[0]):
        resid = images - matmul_high(theta, vecs)
        resid_images = node_mask[None, :] * (degree[None, :] * resid - graph_product(resid))
        stacked = jnp.concatenate([vecs, resid, steps], 0)
        stacked_images = jnp.concatenate([images, resid_images, step_images], 0)
        rotation = rotations[turn]
        new_vecs = matmul_high(rotation, stacked)
        new_images = matmul_high(rotation, stacked_images)
        gram_x, gram_ax = gram_sums(new_vecs, new_images)
        new_steps = matmul_high(rotation[:, vec_count:], stacked[vec_count:])
        new_step_images = matmul_high(rotation[:, vec_count:], stacked_images[vec_count:])
        vecs, images, steps, step_images, theta = settle(
            new_vecs, new_images, new_steps, new_step_images, gram_x, gram_ax, node_total
        )
    return (vecs, theta)


def solution(mesh):
    in_specs = (
        P("row", "col", None, None, None),
        P("row", "col", None, None),
        P("row", "col"),
        P(("row", "col")),
        P(None, ("row", "col")),
        P(),
    )
    out_specs = (P(None, ("row", "col")), P())
    return jax.shard_map(body, mesh=mesh, in_specs=in_specs, out_specs=out_specs, check_vma=False)
```

```python
import jax
import jax.numpy as jnp
from jax import lax
from jax.sharding import PartitionSpec as P


def matmul_high(left, right):
    return jnp.dot(left, right, precision=lax.Precision.HIGHEST)


def lower_inverse(lower_factor):
    order_size = lower_factor.shape[0]
    assert order_size <= 8
    identity = jnp.eye(order_size, dtype=lower_factor.dtype)
    diagonal = jnp.diagonal(lower_factor)
    strict = lower_factor / diagonal[:, None] - identity
    square = matmul_high(strict, strict)
    fourth = matmul_high(square, square)
    inverse = matmul_high(matmul_high(identity - strict, identity + square), identity + fourth)
    return inverse / diagonal[None, :]


def settle(new_vecs, new_images, new_steps, step_images, gram_x, gram_ax, node_total):
    lower_factor = jnp.linalg.cholesky(gram_x / node_total)
    inverse = lower_inverse(lower_factor)
    theta = matmul_high(matmul_high(inverse, gram_ax / node_total), inverse.T)
    return (
        matmul_high(inverse, new_vecs),
        matmul_high(inverse, new_images),
        matmul_high(inverse, new_steps),
        matmul_high(inverse, step_images),
        theta,
    )


def gather_by_exchange(local, axis):
    count = lax.axis_size(axis)
    copies = jnp.broadcast_to(local[None], (count,) + local.shape)
    held = lax.all_to_all(copies, axis, 0, 0, tiled=True)
    return jnp.swapaxes(held, 0, 1).reshape(local.shape[0], count * local.shape[1])


def scatter_sum_by_exchange(chunks, axis):
    held = lax.all_to_all(chunks, axis, 0, 0, tiled=True)
    return jnp.sum(held, axis=0)


def gram_sums(new_vecs, new_images):
    order = new_vecs.shape[0]
    local = jnp.concatenate(
        [matmul_high(new_vecs, new_vecs.T).reshape(-1), matmul_high(new_images, new_vecs.T).reshape(-1)]
    )
    count = lax.axis_size("row") * lax.axis_size("col")
    copies = jnp.broadcast_to(local[None], (count,) + local.shape)
    held = lax.all_to_all(copies, ("row", "col"), 0, 0, tiled=True)
    total = jnp.sum(held, axis=0)
    return total[: order * order].reshape(order, order), total[order * order :].reshape(order, order)


def block_sums(pick, part_values, owners):
    slots, span = pick.shape
    sums = jnp.einsum(
        "sjb,csu->jcbu",
        pick.reshape(slots, owners, span // owners),
        part_values,
        precision=lax.Precision.HIGHEST,
    )
    return sums.reshape(owners, part_values.shape[0], -1)


def direct_terms(part_tiles, part_rows, part_cols, weight_direct, col_blocks, row_span, owners):
    col_values = jnp.take(col_blocks, part_cols, axis=1)
    direct = (
        jnp.einsum("sut,cst->csu", part_tiles, col_values, preferred_element_type=jnp.float32)
        * weight_direct[None, :, None]
    )
    pick_rows = (part_rows[:, None] == jnp.arange(row_span, dtype=jnp.int32)[None, :]).astype(
        jnp.float32
    )
    return block_sums(pick_rows, direct, owners)


def mirror_terms(part_tiles, part_rows, part_cols, weight_mirror, row_blocks, col_span, owners):
    row_values = jnp.take(row_blocks, part_rows, axis=1)
    mirror = (
        jnp.einsum("sut,csu->cst", part_tiles, row_values, preferred_element_type=jnp.float32)
        * weight_mirror[None, :, None]
    )
    pick_cols = (part_cols[:, None] == jnp.arange(col_span, dtype=jnp.int32)[None, :]).astype(
        jnp.float32
    )
    return block_sums(pick_cols, mirror, owners)


def body(tiles, coords, counts, valid, start, rotations):
    row_count = lax.axis_size("row")
    col_count = lax.axis_size("col")
    row_index = lax.axis_index("row")
    col_index = lax.axis_index("col")
    slot_count = tiles.shape[2]
    tile_side = tiles.shape[3]
    stretch_nodes = valid.shape[0]
    per_stretch = stretch_nodes // tile_side
    row_span = col_count * per_stretch
    col_span = row_count * per_stretch
    node_total = jnp.float32(stretch_nodes * row_count * col_count)
    vec_count = start.shape[0]
    flat_tiles = tiles.reshape(slot_count, tile_side, tile_side)
    block_rows = coords[0, 0, 0]
    block_cols = coords[0, 0, 1]
    live_count = counts[0, 0]
    global_rows = row_index * row_span + block_rows
    global_cols = (
        block_cols // per_stretch * col_count + col_index
    ) * per_stretch + block_cols % per_stretch
    live = (jnp.arange(slot_count, dtype=jnp.int32) < live_count).astype(jnp.float32)
    mirror_weight = live * (global_rows != global_cols).astype(jnp.float32)

    def graph_product(vectors):
        width = vectors.shape[0]
        short = vectors.astype(jnp.bfloat16)
        col_side = gather_by_exchange(short, "row")
        col_blocks = col_side.reshape(width, col_span, tile_side)
        rows_total = direct_terms(
            flat_tiles, block_rows, block_cols, live, col_blocks, row_span, col_count
        )
        copies = jnp.broadcast_to(short.astype(jnp.float32)[None], (col_count,) + short.shape)
        held = lax.all_to_all(
            jnp.concatenate([rows_total, copies], axis=1), "col", 0, 0, tiled=True
        )
        direct_part = jnp.sum(held[:, :width], axis=0)
        row_side = jnp.swapaxes(held[:, width:].astype(jnp.bfloat16), 0, 1)
        row_blocks = row_side.reshape(width, row_span, tile_side)
        cols_total = mirror_terms(
            flat_tiles, block_rows, block_cols, mirror_weight, row_blocks, col_span, row_count
        )
        mirror_part = scatter_sum_by_exchange(cols_total, "row")
        return direct_part + mirror_part

    node_mask = valid.astype(jnp.float32)
    first_vecs = start * node_mask[None, :]
    raw = graph_product(jnp.concatenate([node_mask[None, :], first_vecs], 0))
    degree = raw[0]
    first_images = node_mask[None, :] * (degree[None, :] * first_vecs - raw[1:])
    zero_steps = jnp.zeros_like(first_vecs)
    gram_x, gram_ax = gram_sums(first_vecs, first_images)
    vecs, images, steps, step_images, theta = settle(
        first_vecs, first_images, zero_steps, zero_steps, gram_x, gram_ax, node_total
    )
    for turn in range(rotations.shape[0]):
        resid = images - matmul_high(theta, vecs)
        resid_images = node_mask[None, :] * (degree[None, :] * resid - graph_product(resid))
        stacked = jnp.concatenate([vecs, resid, steps], 0)
        stacked_images = jnp.concatenate([images, resid_images, step_images], 0)
        rotation = rotations[turn]
        new_vecs = matmul_high(rotation, stacked)
        new_images = matmul_high(rotation, stacked_images)
        gram_x, gram_ax = gram_sums(new_vecs, new_images)
        new_steps = matmul_high(rotation[:, vec_count:], stacked[vec_count:])
        new_step_images = matmul_high(rotation[:, vec_count:], stacked_images[vec_count:])
        vecs, images, steps, step_images, theta = settle(
            new_vecs, new_images, new_steps, new_step_images, gram_x, gram_ax, node_total
        )
    return (vecs, theta)


def solution(mesh):
    in_specs = (
        P("row", "col", None, None, None),
        P("row", "col", None, None),
        P("row", "col"),
        P(("row", "col")),
        P(None, ("row", "col")),
        P(),
    )
    out_specs = (P(None, ("row", "col")), P())
    return jax.shard_map(body, mesh=mesh, in_specs=in_specs, out_specs=out_specs, check_vma=False)
```

```python
import jax
import jax.numpy as jnp
from jax import lax
from jax.sharding import PartitionSpec as P


def matmul_high(left, right):
    return jnp.dot(left, right, precision=lax.Precision.HIGHEST)


def lower_inverse(lower_factor):
    order_size = lower_factor.shape[0]
    assert order_size <= 8
    identity = jnp.eye(order_size, dtype=lower_factor.dtype)
    diagonal = jnp.diagonal(lower_factor)
    strict = lower_factor / diagonal[:, None] - identity
    square = matmul_high(strict, strict)
    fourth = matmul_high(square, square)
    inverse = matmul_high(matmul_high(identity - strict, identity + square), identity + fourth)
    return inverse / diagonal[None, :]


def settle(new_vecs, new_images, new_steps, step_images, gram_x, gram_ax, node_total):
    lower_factor = jnp.linalg.cholesky(gram_x / node_total)
    inverse = lower_inverse(lower_factor)
    theta = matmul_high(matmul_high(inverse, gram_ax / node_total), inverse.T)
    return (
        matmul_high(inverse, new_vecs),
        matmul_high(inverse, new_images),
        matmul_high(inverse, new_steps),
        matmul_high(inverse, step_images),
        theta,
    )


def gather_by_exchange(local, axis):
    count = lax.axis_size(axis)
    copies = jnp.broadcast_to(local[None], (count,) + local.shape)
    held = lax.all_to_all(copies, axis, 0, 0, tiled=True)
    return jnp.swapaxes(held, 0, 1).reshape(local.shape[0], count * local.shape[1])


def scatter_sum_by_exchange(chunks, axis):
    held = lax.all_to_all(chunks, axis, 0, 0, tiled=True)
    return jnp.sum(held, axis=0)


def sum_by_exchange(local, axis):
    count = lax.axis_size(axis)
    copies = jnp.broadcast_to(local[None], (count,) + local.shape)
    return jnp.sum(lax.all_to_all(copies, axis, 0, 0, tiled=True), axis=0)


def gram_sums(new_vecs, new_images):
    order = new_vecs.shape[0]
    local = jnp.concatenate(
        [matmul_high(new_vecs, new_vecs.T).reshape(-1), matmul_high(new_images, new_vecs.T).reshape(-1)]
    )
    total = sum_by_exchange(sum_by_exchange(local, "row"), "col")
    return total[: order * order].reshape(order, order), total[order * order :].reshape(order, order)


def block_sums(pick, part_values, owners):
    slots, span = pick.shape
    sums = jnp.einsum(
        "sjb,csu->jcbu",
        pick.reshape(slots, owners, span // owners),
        part_values,
        precision=lax.Precision.HIGHEST,
    )
    return sums.reshape(owners, part_values.shape[0], -1)


def direct_terms(part_tiles, part_rows, part_cols, weight_direct, col_blocks, row_span, owners):
    col_values = jnp.take(col_blocks, part_cols, axis=1)
    direct = (
        jnp.einsum("sut,cst->csu", part_tiles, col_values, preferred_element_type=jnp.float32)
        * weight_direct[None, :, None]
    )
    pick_rows = (part_rows[:, None] == jnp.arange(row_span, dtype=jnp.int32)[None, :]).astype(
        jnp.float32
    )
    return block_sums(pick_rows, direct, owners)


def mirror_terms(part_tiles, part_rows, part_cols, weight_mirror, row_blocks, col_span, owners):
    row_values = jnp.take(row_blocks, part_rows, axis=1)
    mirror = (
        jnp.einsum("sut,csu->cst", part_tiles, row_values, preferred_element_type=jnp.float32)
        * weight_mirror[None, :, None]
    )
    pick_cols = (part_cols[:, None] == jnp.arange(col_span, dtype=jnp.int32)[None, :]).astype(
        jnp.float32
    )
    return block_sums(pick_cols, mirror, owners)


def body(tiles, coords, counts, valid, start, rotations):
    row_count = lax.axis_size("row")
    col_count = lax.axis_size("col")
    row_index = lax.axis_index("row")
    col_index = lax.axis_index("col")
    slot_count = tiles.shape[2]
    tile_side = tiles.shape[3]
    stretch_nodes = valid.shape[0]
    per_stretch = stretch_nodes // tile_side
    row_span = col_count * per_stretch
    col_span = row_count * per_stretch
    node_total = jnp.float32(stretch_nodes * row_count * col_count)
    vec_count = start.shape[0]
    flat_tiles = tiles.reshape(slot_count, tile_side, tile_side)
    block_rows = coords[0, 0, 0]
    block_cols = coords[0, 0, 1]
    live_count = counts[0, 0]
    global_rows = row_index * row_span + block_rows
    global_cols = (
        block_cols // per_stretch * col_count + col_index
    ) * per_stretch + block_cols % per_stretch
    live = (jnp.arange(slot_count, dtype=jnp.int32) < live_count).astype(jnp.float32)
    mirror_weight = live * (global_rows != global_cols).astype(jnp.float32)

    def graph_product(vectors):
        width = vectors.shape[0]
        short = vectors.astype(jnp.bfloat16)
        col_side = gather_by_exchange(short, "row")
        col_blocks = col_side.reshape(width, col_span, tile_side)
        rows_total = direct_terms(
            flat_tiles, block_rows, block_cols, live, col_blocks, row_span, col_count
        )
        row_side = gather_by_exchange(short, "col")
        rows_total, row_side = lax.optimization_barrier((rows_total, row_side))
        row_blocks = row_side.reshape(width, row_span, tile_side)
        cols_total = mirror_terms(
            flat_tiles, block_rows, block_cols, mirror_weight, row_blocks, col_span, row_count
        )
        direct_part = scatter_sum_by_exchange(rows_total, "col")
        direct_part, cols_total = lax.optimization_barrier((direct_part, cols_total))
        mirror_part = scatter_sum_by_exchange(cols_total, "row")
        return direct_part + mirror_part

    node_mask = valid.astype(jnp.float32)
    first_vecs = start * node_mask[None, :]
    raw = graph_product(jnp.concatenate([node_mask[None, :], first_vecs], 0))
    degree = raw[0]
    first_images = node_mask[None, :] * (degree[None, :] * first_vecs - raw[1:])
    zero_steps = jnp.zeros_like(first_vecs)
    gram_x, gram_ax = gram_sums(first_vecs, first_images)
    vecs, images, steps, step_images, theta = settle(
        first_vecs, first_images, zero_steps, zero_steps, gram_x, gram_ax, node_total
    )
    for turn in range(rotations.shape[0]):
        resid = images - matmul_high(theta, vecs)
        resid_images = node_mask[None, :] * (degree[None, :] * resid - graph_product(resid))
        stacked = jnp.concatenate([vecs, resid, steps], 0)
        stacked_images = jnp.concatenate([images, resid_images, step_images], 0)
        rotation = rotations[turn]
        new_vecs = matmul_high(rotation, stacked)
        new_images = matmul_high(rotation, stacked_images)
        gram_x, gram_ax = gram_sums(new_vecs, new_images)
        new_steps = matmul_high(rotation[:, vec_count:], stacked[vec_count:])
        new_step_images = matmul_high(rotation[:, vec_count:], stacked_images[vec_count:])
        vecs, images, steps, step_images, theta = settle(
            new_vecs, new_images, new_steps, new_step_images, gram_x, gram_ax, node_total
        )
    return (vecs, theta)


def solution(mesh):
    in_specs = (
        P("row", "col", None, None, None),
        P("row", "col", None, None),
        P("row", "col"),
        P(("row", "col")),
        P(None, ("row", "col")),
        P(),
    )
    out_specs = (P(None, ("row", "col")), P())
    return jax.shard_map(body, mesh=mesh, in_specs=in_specs, out_specs=out_specs, check_vma=False)
```

```python
import jax
import jax.numpy as jnp
from jax import lax
from jax.sharding import PartitionSpec as P


def matmul_high(left, right):
    return jnp.dot(left, right, precision=lax.Precision.HIGHEST)


def lower_inverse(lower_factor):
    order_size = lower_factor.shape[0]
    assert order_size <= 8
    identity = jnp.eye(order_size, dtype=lower_factor.dtype)
    diagonal = jnp.diagonal(lower_factor)
    strict = lower_factor / diagonal[:, None] - identity
    square = matmul_high(strict, strict)
    fourth = matmul_high(square, square)
    inverse = matmul_high(matmul_high(identity - strict, identity + square), identity + fourth)
    return inverse / diagonal[None, :]


def settle(new_vecs, new_images, new_steps, step_images, gram_x, gram_ax, node_total):
    lower_factor = jnp.linalg.cholesky(gram_x / node_total)
    inverse = lower_inverse(lower_factor)
    theta = matmul_high(matmul_high(inverse, gram_ax / node_total), inverse.T)
    return (
        matmul_high(inverse, new_vecs),
        matmul_high(inverse, new_images),
        matmul_high(inverse, new_steps),
        matmul_high(inverse, step_images),
        theta,
    )


def dense_rows(chunks):
    peers, rows, nodes = chunks.shape
    if rows % 8 == 0:
        return chunks
    return chunks.reshape(peers, rows * nodes // 128, 128)


def gather_by_exchange(local, axis):
    count = lax.axis_size(axis)
    copies = jnp.broadcast_to(local[None], (count,) + local.shape)
    held = lax.all_to_all(dense_rows(copies), axis, 0, 0, tiled=True).reshape(copies.shape)
    return jnp.swapaxes(held, 0, 1).reshape(local.shape[0], count * local.shape[1])


def scatter_sum_by_exchange(chunks, axis):
    held = lax.all_to_all(dense_rows(chunks), axis, 0, 0, tiled=True)
    return jnp.sum(held, axis=0).reshape(chunks.shape[1:])


def gram_sums(new_vecs, new_images):
    order = new_vecs.shape[0]
    local = jnp.concatenate(
        [matmul_high(new_vecs, new_vecs.T).reshape(-1), matmul_high(new_images, new_vecs.T).reshape(-1)]
    )
    count = lax.axis_size("row") * lax.axis_size("col")
    copies = jnp.broadcast_to(local[None], (count,) + local.shape)
    held = lax.all_to_all(copies, ("row", "col"), 0, 0, tiled=True)
    total = jnp.sum(held, axis=0)
    return total[: order * order].reshape(order, order), total[order * order :].reshape(order, order)


def block_sums(pick, part_values, owners):
    slots, span = pick.shape
    sums = jnp.einsum(
        "sjb,csu->jcbu",
        pick.reshape(slots, owners, span // owners),
        part_values,
        precision=lax.Precision.HIGHEST,
    )
    return sums.reshape(owners, part_values.shape[0], -1)


def direct_terms(part_tiles, part_rows, part_cols, weight_direct, col_blocks, row_span, owners):
    col_values = jnp.take(col_blocks, part_cols, axis=1)
    direct = (
        jnp.einsum("sut,cst->csu", part_tiles, col_values, preferred_element_type=jnp.float32)
        * weight_direct[None, :, None]
    )
    pick_rows = (part_rows[:, None] == jnp.arange(row_span, dtype=jnp.int32)[None, :]).astype(
        jnp.float32
    )
    return block_sums(pick_rows, direct, owners)


def mirror_terms(part_tiles, part_rows, part_cols, weight_mirror, row_blocks, col_span, owners):
    row_values = jnp.take(row_blocks, part_rows, axis=1)
    mirror = (
        jnp.einsum("sut,csu->cst", part_tiles, row_values, preferred_element_type=jnp.float32)
        * weight_mirror[None, :, None]
    )
    pick_cols = (part_cols[:, None] == jnp.arange(col_span, dtype=jnp.int32)[None, :]).astype(
        jnp.float32
    )
    return block_sums(pick_cols, mirror, owners)


def body(tiles, coords, counts, valid, start, rotations):
    row_count = lax.axis_size("row")
    col_count = lax.axis_size("col")
    row_index = lax.axis_index("row")
    col_index = lax.axis_index("col")
    slot_count = tiles.shape[2]
    tile_side = tiles.shape[3]
    stretch_nodes = valid.shape[0]
    per_stretch = stretch_nodes // tile_side
    row_span = col_count * per_stretch
    col_span = row_count * per_stretch
    node_total = jnp.float32(stretch_nodes * row_count * col_count)
    vec_count = start.shape[0]
    flat_tiles = tiles.reshape(slot_count, tile_side, tile_side)
    block_rows = coords[0, 0, 0]
    block_cols = coords[0, 0, 1]
    live_count = counts[0, 0]
    global_rows = row_index * row_span + block_rows
    global_cols = (
        block_cols // per_stretch * col_count + col_index
    ) * per_stretch + block_cols % per_stretch
    live = (jnp.arange(slot_count, dtype=jnp.int32) < live_count).astype(jnp.float32)
    mirror_weight = live * (global_rows != global_cols).astype(jnp.float32)

    def graph_product(vectors):
        width = vectors.shape[0]
        short = vectors.astype(jnp.bfloat16)
        col_side = gather_by_exchange(short, "row")
        col_blocks = col_side.reshape(width, col_span, tile_side)
        rows_total = direct_terms(
            flat_tiles, block_rows, block_cols, live, col_blocks, row_span, col_count
        )
        row_side = gather_by_exchange(short, "col")
        rows_total, row_side = lax.optimization_barrier((rows_total, row_side))
        row_blocks = row_side.reshape(width, row_span, tile_side)
        cols_total = mirror_terms(
            flat_tiles, block_rows, block_cols, mirror_weight, row_blocks, col_span, row_count
        )
        direct_part = scatter_sum_by_exchange(rows_total, "col")
        direct_part, cols_total = lax.optimization_barrier((direct_part, cols_total))
        mirror_part = scatter_sum_by_exchange(cols_total, "row")
        return direct_part + mirror_part

    node_mask = valid.astype(jnp.float32)
    first_vecs = start * node_mask[None, :]
    raw = graph_product(jnp.concatenate([node_mask[None, :], first_vecs], 0))
    degree = raw[0]
    first_images = node_mask[None, :] * (degree[None, :] * first_vecs - raw[1:])
    zero_steps = jnp.zeros_like(first_vecs)
    gram_x, gram_ax = gram_sums(first_vecs, first_images)
    vecs, images, steps, step_images, theta = settle(
        first_vecs, first_images, zero_steps, zero_steps, gram_x, gram_ax, node_total
    )
    for turn in range(rotations.shape[0]):
        resid = images - matmul_high(theta, vecs)
        resid_images = node_mask[None, :] * (degree[None, :] * resid - graph_product(resid))
        stacked = jnp.concatenate([vecs, resid, steps], 0)
        stacked_images = jnp.concatenate([images, resid_images, step_images], 0)
        rotation = rotations[turn]
        new_vecs = matmul_high(rotation, stacked)
        new_images = matmul_high(rotation, stacked_images)
        gram_x, gram_ax = gram_sums(new_vecs, new_images)
        new_steps = matmul_high(rotation[:, vec_count:], stacked[vec_count:])
        new_step_images = matmul_high(rotation[:, vec_count:], stacked_images[vec_count:])
        vecs, images, steps, step_images, theta = settle(
            new_vecs, new_images, new_steps, new_step_images, gram_x, gram_ax, node_total
        )
    return (vecs, theta)


def solution(mesh):
    in_specs = (
        P("row", "col", None, None, None),
        P("row", "col", None, None),
        P("row", "col"),
        P(("row", "col")),
        P(None, ("row", "col")),
        P(),
    )
    out_specs = (P(None, ("row", "col")), P())
    return jax.shard_map(body, mesh=mesh, in_specs=in_specs, out_specs=out_specs, check_vma=False)
```

```python
import jax
import jax.numpy as jnp
from jax import lax
from jax.sharding import PartitionSpec as P


def matmul_high(left, right):
    return jnp.dot(left, right, precision=lax.Precision.HIGHEST)


def lower_inverse(lower_factor):
    order_size = lower_factor.shape[0]
    assert order_size <= 8
    identity = jnp.eye(order_size, dtype=lower_factor.dtype)
    diagonal = jnp.diagonal(lower_factor)
    strict = lower_factor / diagonal[:, None] - identity
    square = matmul_high(strict, strict)
    fourth = matmul_high(square, square)
    inverse = matmul_high(matmul_high(identity - strict, identity + square), identity + fourth)
    return inverse / diagonal[None, :]


def settle(new_vecs, new_images, new_steps, step_images, gram_x, gram_ax, node_total):
    lower_factor = jnp.linalg.cholesky(gram_x / node_total)
    inverse = lower_inverse(lower_factor)
    theta = matmul_high(matmul_high(inverse, gram_ax / node_total), inverse.T)
    return (
        matmul_high(inverse, new_vecs),
        matmul_high(inverse, new_images),
        matmul_high(inverse, new_steps),
        matmul_high(inverse, step_images),
        theta,
    )


def dense_rows(chunks):
    peers, rows, nodes = chunks.shape
    if rows % (32 // chunks.dtype.itemsize) == 0:
        return chunks
    return chunks.reshape(peers, rows * nodes // 128, 128)


def gather_by_exchange(local, axis):
    count = lax.axis_size(axis)
    copies = jnp.broadcast_to(local[None], (count,) + local.shape)
    held = lax.all_to_all(dense_rows(copies), axis, 0, 0, tiled=True).reshape(copies.shape)
    return jnp.swapaxes(held, 0, 1).reshape(local.shape[0], count * local.shape[1])


def scatter_sum_by_exchange(chunks, axis):
    held = lax.all_to_all(dense_rows(chunks), axis, 0, 0, tiled=True)
    return jnp.sum(held, axis=0).reshape(chunks.shape[1:])


def gram_sums(new_vecs, new_images):
    order = new_vecs.shape[0]
    local = jnp.concatenate(
        [matmul_high(new_vecs, new_vecs.T).reshape(-1), matmul_high(new_images, new_vecs.T).reshape(-1)]
    )
    count = lax.axis_size("row") * lax.axis_size("col")
    copies = jnp.broadcast_to(local[None], (count,) + local.shape)
    held = lax.all_to_all(copies, ("row", "col"), 0, 0, tiled=True)
    total = jnp.sum(held, axis=0)
    return total[: order * order].reshape(order, order), total[order * order :].reshape(order, order)


def block_sums(pick, part_values, owners):
    slots, span = pick.shape
    sums = jnp.einsum(
        "sjb,csu->jcbu",
        pick.reshape(slots, owners, span // owners),
        part_values,
        precision=lax.Precision.HIGHEST,
    )
    return sums.reshape(owners, part_values.shape[0], -1)


def direct_terms(part_tiles, part_rows, part_cols, weight_direct, col_blocks, row_span, owners):
    col_values = jnp.take(col_blocks, part_cols, axis=1)
    direct = (
        jnp.einsum("sut,cst->csu", part_tiles, col_values, preferred_element_type=jnp.float32)
        * weight_direct[None, :, None]
    )
    pick_rows = (part_rows[:, None] == jnp.arange(row_span, dtype=jnp.int32)[None, :]).astype(
        jnp.float32
    )
    return block_sums(pick_rows, direct, owners)


def mirror_terms(part_tiles, part_rows, part_cols, weight_mirror, row_blocks, col_span, owners):
    row_values = jnp.take(row_blocks, part_rows, axis=1)
    mirror = (
        jnp.einsum("sut,csu->cst", part_tiles, row_values, preferred_element_type=jnp.float32)
        * weight_mirror[None, :, None]
    )
    pick_cols = (part_cols[:, None] == jnp.arange(col_span, dtype=jnp.int32)[None, :]).astype(
        jnp.float32
    )
    return block_sums(pick_cols, mirror, owners)


def body(tiles, coords, counts, valid, start, rotations):
    row_count = lax.axis_size("row")
    col_count = lax.axis_size("col")
    row_index = lax.axis_index("row")
    col_index = lax.axis_index("col")
    slot_count = tiles.shape[2]
    tile_side = tiles.shape[3]
    stretch_nodes = valid.shape[0]
    per_stretch = stretch_nodes // tile_side
    row_span = col_count * per_stretch
    col_span = row_count * per_stretch
    node_total = jnp.float32(stretch_nodes * row_count * col_count)
    vec_count = start.shape[0]
    flat_tiles = tiles.reshape(slot_count, tile_side, tile_side)
    block_rows = coords[0, 0, 0]
    block_cols = coords[0, 0, 1]
    live_count = counts[0, 0]
    global_rows = row_index * row_span + block_rows
    global_cols = (
        block_cols // per_stretch * col_count + col_index
    ) * per_stretch + block_cols % per_stretch
    live = (jnp.arange(slot_count, dtype=jnp.int32) < live_count).astype(jnp.float32)
    mirror_weight = live * (global_rows != global_cols).astype(jnp.float32)

    def graph_product(vectors):
        width = vectors.shape[0]
        short = vectors.astype(jnp.bfloat16)
        col_side = gather_by_exchange(short, "row")
        col_blocks = col_side.reshape(width, col_span, tile_side)
        rows_total = direct_terms(
            flat_tiles, block_rows, block_cols, live, col_blocks, row_span, col_count
        )
        row_side = gather_by_exchange(short, "col")
        rows_total, row_side = lax.optimization_barrier((rows_total, row_side))
        row_blocks = row_side.reshape(width, row_span, tile_side)
        cols_total = mirror_terms(
            flat_tiles, block_rows, block_cols, mirror_weight, row_blocks, col_span, row_count
        )
        direct_part = scatter_sum_by_exchange(rows_total, "col")
        direct_part, cols_total = lax.optimization_barrier((direct_part, cols_total))
        mirror_part = scatter_sum_by_exchange(cols_total, "row")
        return direct_part + mirror_part

    node_mask = valid.astype(jnp.float32)
    first_vecs = start * node_mask[None, :]
    raw = graph_product(jnp.concatenate([node_mask[None, :], first_vecs], 0))
    degree = raw[0]
    first_images = node_mask[None, :] * (degree[None, :] * first_vecs - raw[1:])
    zero_steps = jnp.zeros_like(first_vecs)
    gram_x, gram_ax = gram_sums(first_vecs, first_images)
    vecs, images, steps, step_images, theta = settle(
        first_vecs, first_images, zero_steps, zero_steps, gram_x, gram_ax, node_total
    )
    for turn in range(rotations.shape[0]):
        resid = images - matmul_high(theta, vecs)
        resid_images = node_mask[None, :] * (degree[None, :] * resid - graph_product(resid))
        stacked = jnp.concatenate([vecs, resid, steps], 0)
        stacked_images = jnp.concatenate([images, resid_images, step_images], 0)
        rotation = rotations[turn]
        new_vecs = matmul_high(rotation, stacked)
        new_images = matmul_high(rotation, stacked_images)
        gram_x, gram_ax = gram_sums(new_vecs, new_images)
        new_steps = matmul_high(rotation[:, vec_count:], stacked[vec_count:])
        new_step_images = matmul_high(rotation[:, vec_count:], stacked_images[vec_count:])
        vecs, images, steps, step_images, theta = settle(
            new_vecs, new_images, new_steps, new_step_images, gram_x, gram_ax, node_total
        )
    return (vecs, theta)


def solution(mesh):
    in_specs = (
        P("row", "col", None, None, None),
        P("row", "col", None, None),
        P("row", "col"),
        P(("row", "col")),
        P(None, ("row", "col")),
        P(),
    )
    out_specs = (P(None, ("row", "col")), P())
    return jax.shard_map(body, mesh=mesh, in_specs=in_specs, out_specs=out_specs, check_vma=False)
```

```python
import jax
import jax.numpy as jnp
from jax import lax
from jax.sharding import PartitionSpec as P


def matmul_high(left, right):
    return jnp.dot(left, right, precision=lax.Precision.HIGHEST)


def lower_inverse(lower_factor):
    order_size = lower_factor.shape[0]
    assert order_size <= 8
    identity = jnp.eye(order_size, dtype=lower_factor.dtype)
    diagonal = jnp.sum(lower_factor * identity, axis=1)
    strict = lower_factor / diagonal[:, None] - identity
    square = matmul_high(strict, strict)
    fourth = matmul_high(square, square)
    inverse = matmul_high(matmul_high(identity - strict, identity + square), identity + fourth)
    return inverse / diagonal[None, :]


def settle(new_vecs, new_images, new_steps, step_images, gram_x, gram_ax, node_total):
    lower_factor = jnp.linalg.cholesky(gram_x / node_total)
    inverse = lower_inverse(lower_factor)
    theta = matmul_high(matmul_high(inverse, gram_ax / node_total), inverse.T)
    return (
        matmul_high(inverse, new_vecs),
        matmul_high(inverse, new_images),
        matmul_high(inverse, new_steps),
        matmul_high(inverse, step_images),
        theta,
    )


def dense_rows(chunks):
    peers, rows, nodes = chunks.shape
    if rows % 8 == 0:
        return chunks
    return chunks.reshape(peers, rows * nodes // 128, 128)


def gather_by_exchange(local, axis):
    count = lax.axis_size(axis)
    copies = jnp.broadcast_to(local[None], (count,) + local.shape)
    held = lax.all_to_all(dense_rows(copies), axis, 0, 0, tiled=True).reshape(copies.shape)
    return jnp.swapaxes(held, 0, 1).reshape(local.shape[0], count * local.shape[1])


def scatter_sum_by_exchange(chunks, axis):
    held = lax.all_to_all(dense_rows(chunks), axis, 0, 0, tiled=True)
    return jnp.sum(held, axis=0).reshape(chunks.shape[1:])


def gram_sums(new_vecs, new_images):
    order = new_vecs.shape[0]
    local = jnp.concatenate(
        [matmul_high(new_vecs, new_vecs.T).reshape(-1), matmul_high(new_images, new_vecs.T).reshape(-1)]
    )
    count = lax.axis_size("row") * lax.axis_size("col")
    copies = jnp.broadcast_to(local[None], (count,) + local.shape)
    held = lax.all_to_all(copies, ("row", "col"), 0, 0, tiled=True)
    total = jnp.sum(held, axis=0)
    return total[: order * order].reshape(order, order), total[order * order :].reshape(order, order)


def block_sums(pick, part_values, owners):
    slots, span = pick.shape
    sums = jnp.einsum(
        "sjb,csu->jcbu",
        pick.reshape(slots, owners, span // owners),
        part_values,
        precision=lax.Precision.HIGHEST,
    )
    return sums.reshape(owners, part_values.shape[0], -1)


def direct_terms(part_tiles, part_rows, part_cols, weight_direct, col_blocks, row_span, owners):
    col_values = jnp.take(col_blocks, part_cols, axis=1)
    direct = (
        jnp.einsum("sut,cst->csu", part_tiles, col_values, preferred_element_type=jnp.float32)
        * weight_direct[None, :, None]
    )
    pick_rows = (part_rows[:, None] == jnp.arange(row_span, dtype=jnp.int32)[None, :]).astype(
        jnp.float32
    )
    return block_sums(pick_rows, direct, owners)


def mirror_terms(part_tiles, part_rows, part_cols, weight_mirror, row_blocks, col_span, owners):
    row_values = jnp.take(row_blocks, part_rows, axis=1)
    mirror = (
        jnp.einsum("sut,csu->cst", part_tiles, row_values, preferred_element_type=jnp.float32)
        * weight_mirror[None, :, None]
    )
    pick_cols = (part_cols[:, None] == jnp.arange(col_span, dtype=jnp.int32)[None, :]).astype(
        jnp.float32
    )
    return block_sums(pick_cols, mirror, owners)


def body(tiles, coords, counts, valid, start, rotations):
    row_count = lax.axis_size("row")
    col_count = lax.axis_size("col")
    row_index = lax.axis_index("row")
    col_index = lax.axis_index("col")
    slot_count = tiles.shape[2]
    tile_side = tiles.shape[3]
    stretch_nodes = valid.shape[0]
    per_stretch = stretch_nodes // tile_side
    row_span = col_count * per_stretch
    col_span = row_count * per_stretch
    node_total = jnp.float32(stretch_nodes * row_count * col_count)
    vec_count = start.shape[0]
    flat_tiles = tiles.reshape(slot_count, tile_side, tile_side)
    block_rows = coords[0, 0, 0]
    block_cols = coords[0, 0, 1]
    live_count = counts[0, 0]
    global_rows = row_index * row_span + block_rows
    global_cols = (
        block_cols // per_stretch * col_count + col_index
    ) * per_stretch + block_cols % per_stretch
    live = (jnp.arange(slot_count, dtype=jnp.int32) < live_count).astype(jnp.float32)
    mirror_weight = live * (global_rows != global_cols).astype(jnp.float32)

    def graph_product(vectors):
        width = vectors.shape[0]
        short = vectors.astype(jnp.bfloat16)
        col_side = gather_by_exchange(short, "row")
        col_blocks = col_side.reshape(width, col_span, tile_side)
        rows_total = direct_terms(
            flat_tiles, block_rows, block_cols, live, col_blocks, row_span, col_count
        )
        row_side = gather_by_exchange(short, "col")
        rows_total, row_side = lax.optimization_barrier((rows_total, row_side))
        row_blocks = row_side.reshape(width, row_span, tile_side)
        cols_total = mirror_terms(
            flat_tiles, block_rows, block_cols, mirror_weight, row_blocks, col_span, row_count
        )
        direct_part = scatter_sum_by_exchange(rows_total, "col")
        direct_part, cols_total = lax.optimization_barrier((direct_part, cols_total))
        mirror_part = scatter_sum_by_exchange(cols_total, "row")
        return direct_part + mirror_part

    node_mask = valid.astype(jnp.float32)
    first_vecs = start * node_mask[None, :]
    raw = graph_product(jnp.concatenate([node_mask[None, :], first_vecs], 0))
    degree = raw[0]
    first_images = node_mask[None, :] * (degree[None, :] * first_vecs - raw[1:])
    zero_steps = jnp.zeros_like(first_vecs)
    gram_x, gram_ax = gram_sums(first_vecs, first_images)
    vecs, images, steps, step_images, theta = settle(
        first_vecs, first_images, zero_steps, zero_steps, gram_x, gram_ax, node_total
    )
    for turn in range(rotations.shape[0]):
        resid = images - matmul_high(theta, vecs)
        resid_images = node_mask[None, :] * (degree[None, :] * resid - graph_product(resid))
        stacked = jnp.concatenate([vecs, resid, steps], 0)
        stacked_images = jnp.concatenate([images, resid_images, step_images], 0)
        rotation = rotations[turn]
        new_vecs = matmul_high(rotation, stacked)
        new_images = matmul_high(rotation, stacked_images)
        gram_x, gram_ax = gram_sums(new_vecs, new_images)
        new_steps = matmul_high(rotation[:, vec_count:], stacked[vec_count:])
        new_step_images = matmul_high(rotation[:, vec_count:], stacked_images[vec_count:])
        vecs, images, steps, step_images, theta = settle(
            new_vecs, new_images, new_steps, new_step_images, gram_x, gram_ax, node_total
        )
    return (vecs, theta)


def solution(mesh):
    in_specs = (
        P("row", "col", None, None, None),
        P("row", "col", None, None),
        P("row", "col"),
        P(("row", "col")),
        P(None, ("row", "col")),
        P(),
    )
    out_specs = (P(None, ("row", "col")), P())
    return jax.shard_map(body, mesh=mesh, in_specs=in_specs, out_specs=out_specs, check_vma=False)
```

```python
import jax
import jax.numpy as jnp
from jax import lax
from jax.sharding import PartitionSpec as P


def matmul_high(left, right):
    return jnp.dot(left, right, precision=lax.Precision.HIGHEST)


def lower_inverse(lower_factor):
    order_size = lower_factor.shape[0]
    assert order_size <= 8
    identity = jnp.eye(order_size, dtype=lower_factor.dtype)
    diagonal = jnp.diagonal(lower_factor)
    strict = lower_factor / diagonal[:, None] - identity
    square = matmul_high(strict, strict)
    fourth = matmul_high(square, square)
    inverse = matmul_high(matmul_high(identity - strict, identity + square), identity + fourth)
    return inverse / diagonal[None, :]


def settle(new_vecs, new_images, new_steps, step_images, gram_x, gram_ax, node_total):
    lower_factor = jnp.linalg.cholesky(gram_x / node_total)
    inverse = lower_inverse(lower_factor)
    theta = matmul_high(matmul_high(inverse, gram_ax / node_total), inverse.T)
    return (
        matmul_high(inverse, new_vecs),
        matmul_high(inverse, new_images),
        matmul_high(inverse, new_steps),
        matmul_high(inverse, step_images),
        theta,
    )


def dense_rows(chunks):
    peers, rows, nodes = chunks.shape
    if rows % 8 == 0:
        return chunks
    return chunks.reshape(peers, rows * nodes // 128, 128)


def gather_by_exchange(local, axis):
    count = lax.axis_size(axis)
    copies = jnp.broadcast_to(local[None], (count,) + local.shape)
    held = lax.all_to_all(dense_rows(copies), axis, 0, 0, tiled=True).reshape(copies.shape)
    return jnp.swapaxes(held, 0, 1).reshape(local.shape[0], count * local.shape[1])


def scatter_sum_by_exchange(chunks, axis):
    held = lax.all_to_all(dense_rows(chunks), axis, 0, 0, tiled=True)
    return jnp.sum(held, axis=0).reshape(chunks.shape[1:])


def gram_sums(new_vecs, new_images):
    order = new_vecs.shape[0]
    local = jnp.concatenate(
        [matmul_high(new_vecs, new_vecs.T).reshape(-1), matmul_high(new_images, new_vecs.T).reshape(-1)]
    )
    count = lax.axis_size("row") * lax.axis_size("col")
    copies = jnp.broadcast_to(local[None], (count,) + local.shape)
    held = lax.all_to_all(copies, ("col", "row"), 0, 0, tiled=True)
    total = jnp.sum(held, axis=0)
    return total[: order * order].reshape(order, order), total[order * order :].reshape(order, order)


def block_sums(pick, part_values, owners):
    slots, span = pick.shape
    sums = jnp.einsum(
        "sjb,csu->jcbu",
        pick.reshape(slots, owners, span // owners),
        part_values,
        precision=lax.Precision.HIGHEST,
    )
    return sums.reshape(owners, part_values.shape[0], -1)


def direct_terms(part_tiles, part_rows, part_cols, weight_direct, col_blocks, row_span, owners):
    col_values = jnp.take(col_blocks, part_cols, axis=1)
    direct = (
        jnp.einsum("sut,cst->csu", part_tiles, col_values, preferred_element_type=jnp.float32)
        * weight_direct[None, :, None]
    )
    pick_rows = (part_rows[:, None] == jnp.arange(row_span, dtype=jnp.int32)[None, :]).astype(
        jnp.float32
    )
    return block_sums(pick_rows, direct, owners)


def mirror_terms(part_tiles, part_rows, part_cols, weight_mirror, row_blocks, col_span, owners):
    row_values = jnp.take(row_blocks, part_rows, axis=1)
    mirror = (
        jnp.einsum("sut,csu->cst", part_tiles, row_values, preferred_element_type=jnp.float32)
        * weight_mirror[None, :, None]
    )
    pick_cols = (part_cols[:, None] == jnp.arange(col_span, dtype=jnp.int32)[None, :]).astype(
        jnp.float32
    )
    return block_sums(pick_cols, mirror, owners)


def body(tiles, coords, counts, valid, start, rotations):
    row_count = lax.axis_size("row")
    col_count = lax.axis_size("col")
    row_index = lax.axis_index("row")
    col_index = lax.axis_index("col")
    slot_count = tiles.shape[2]
    tile_side = tiles.shape[3]
    stretch_nodes = valid.shape[0]
    per_stretch = stretch_nodes // tile_side
    row_span = col_count * per_stretch
    col_span = row_count * per_stretch
    node_total = jnp.float32(stretch_nodes * row_count * col_count)
    vec_count = start.shape[0]
    flat_tiles = tiles.reshape(slot_count, tile_side, tile_side)
    block_rows = coords[0, 0, 0]
    block_cols = coords[0, 0, 1]
    live_count = counts[0, 0]
    global_rows = row_index * row_span + block_rows
    global_cols = (
        block_cols // per_stretch * col_count + col_index
    ) * per_stretch + block_cols % per_stretch
    live = (jnp.arange(slot_count, dtype=jnp.int32) < live_count).astype(jnp.float32)
    mirror_weight = live * (global_rows != global_cols).astype(jnp.float32)

    def graph_product(vectors):
        width = vectors.shape[0]
        short = vectors.astype(jnp.bfloat16)
        col_side = gather_by_exchange(short, "row")
        col_blocks = col_side.reshape(width, col_span, tile_side)
        rows_total = direct_terms(
            flat_tiles, block_rows, block_cols, live, col_blocks, row_span, col_count
        )
        row_side = gather_by_exchange(short, "col")
        rows_total, row_side = lax.optimization_barrier((rows_total, row_side))
        row_blocks = row_side.reshape(width, row_span, tile_side)
        cols_total = mirror_terms(
            flat_tiles, block_rows, block_cols, mirror_weight, row_blocks, col_span, row_count
        )
        direct_part = scatter_sum_by_exchange(rows_total, "col")
        direct_part, cols_total = lax.optimization_barrier((direct_part, cols_total))
        mirror_part = scatter_sum_by_exchange(cols_total, "row")
        return direct_part + mirror_part

    node_mask = valid.astype(jnp.float32)
    first_vecs = start * node_mask[None, :]
    raw = graph_product(jnp.concatenate([node_mask[None, :], first_vecs], 0))
    degree = raw[0]
    first_images = node_mask[None, :] * (degree[None, :] * first_vecs - raw[1:])
    zero_steps = jnp.zeros_like(first_vecs)
    gram_x, gram_ax = gram_sums(first_vecs, first_images)
    vecs, images, steps, step_images, theta = settle(
        first_vecs, first_images, zero_steps, zero_steps, gram_x, gram_ax, node_total
    )
    for turn in range(rotations.shape[0]):
        resid = images - matmul_high(theta, vecs)
        resid_images = node_mask[None, :] * (degree[None, :] * resid - graph_product(resid))
        stacked = jnp.concatenate([vecs, resid, steps], 0)
        stacked_images = jnp.concatenate([images, resid_images, step_images], 0)
        rotation = rotations[turn]
        new_vecs = matmul_high(rotation, stacked)
        new_images = matmul_high(rotation, stacked_images)
        gram_x, gram_ax = gram_sums(new_vecs, new_images)
        new_steps = matmul_high(rotation[:, vec_count:], stacked[vec_count:])
        new_step_images = matmul_high(rotation[:, vec_count:], stacked_images[vec_count:])
        vecs, images, steps, step_images, theta = settle(
            new_vecs, new_images, new_steps, new_step_images, gram_x, gram_ax, node_total
        )
    return (vecs, theta)


def solution(mesh):
    in_specs = (
        P("row", "col", None, None, None),
        P("row", "col", None, None),
        P("row", "col"),
        P(("row", "col")),
        P(None, ("row", "col")),
        P(),
    )
    out_specs = (P(None, ("row", "col")), P())
    return jax.shard_map(body, mesh=mesh, in_specs=in_specs, out_specs=out_specs, check_vma=False)
```

```python
import jax
import jax.numpy as jnp
from jax import lax
from jax.sharding import PartitionSpec as P


def matmul_high(left, right):
    return jnp.dot(left, right, precision=lax.Precision.HIGHEST)


def lower_inverse(lower_factor):
    order_size = lower_factor.shape[0]
    assert order_size <= 8
    identity = jnp.eye(order_size, dtype=lower_factor.dtype)
    diagonal = jnp.diagonal(lower_factor)
    strict = lower_factor / diagonal[:, None] - identity
    square = matmul_high(strict, strict)
    fourth = matmul_high(square, square)
    inverse = matmul_high(matmul_high(identity - strict, identity + square), identity + fourth)
    return inverse / diagonal[None, :]


def settle(new_vecs, new_images, new_steps, step_images, gram_x, gram_ax, node_total):
    lower_factor = jnp.linalg.cholesky(gram_x / node_total)
    inverse = lower_inverse(lower_factor)
    theta = matmul_high(matmul_high(inverse, gram_ax / node_total), inverse.T)
    return (
        matmul_high(inverse, new_vecs),
        matmul_high(inverse, new_images),
        matmul_high(inverse, new_steps),
        matmul_high(inverse, step_images),
        theta,
    )


def dense_rows(chunks):
    peers, rows, nodes = chunks.shape
    if rows % 8 == 0:
        return chunks
    return chunks.reshape(peers, rows * nodes // 128, 128)


def gather_by_exchange(local, axis):
    count = lax.axis_size(axis)
    copies = jnp.broadcast_to(local[None], (count,) + local.shape)
    held = lax.all_to_all(dense_rows(copies), axis, 0, 0, tiled=True).reshape(copies.shape)
    return jnp.swapaxes(held, 0, 1).reshape(local.shape[0], count * local.shape[1])


def scatter_sum_by_exchange(chunks, axis):
    held = lax.all_to_all(dense_rows(chunks), axis, 0, 0, tiled=True)
    return jnp.sum(held, axis=0).reshape(chunks.shape[1:])


def gram_sums(new_vecs, new_images):
    order = new_vecs.shape[0]
    count = lax.axis_size("row") * lax.axis_size("col")
    parts = [matmul_high(new_vecs, new_vecs.T), matmul_high(new_images, new_vecs.T)]
    copies = jnp.concatenate(
        [jnp.broadcast_to(part.reshape(1, -1), (count, order * order)) for part in parts], axis=1
    )
    held = lax.all_to_all(copies, ("row", "col"), 0, 0, tiled=True)
    total = jnp.sum(held, axis=0)
    return total[: order * order].reshape(order, order), total[order * order :].reshape(order, order)


def block_sums(pick, part_values, owners):
    slots, span = pick.shape
    sums = jnp.einsum(
        "sjb,csu->jcbu",
        pick.reshape(slots, owners, span // owners),
        part_values,
        precision=lax.Precision.HIGHEST,
    )
    return sums.reshape(owners, part_values.shape[0], -1)


def direct_terms(part_tiles, part_rows, part_cols, weight_direct, col_blocks, row_span, owners):
    col_values = jnp.take(col_blocks, part_cols, axis=1)
    direct = (
        jnp.einsum("sut,cst->csu", part_tiles, col_values, preferred_element_type=jnp.float32)
        * weight_direct[None, :, None]
    )
    pick_rows = (part_rows[:, None] == jnp.arange(row_span, dtype=jnp.int32)[None, :]).astype(
        jnp.float32
    )
    return block_sums(pick_rows, direct, owners)


def mirror_terms(part_tiles, part_rows, part_cols, weight_mirror, row_blocks, col_span, owners):
    row_values = jnp.take(row_blocks, part_rows, axis=1)
    mirror = (
        jnp.einsum("sut,csu->cst", part_tiles, row_values, preferred_element_type=jnp.float32)
        * weight_mirror[None, :, None]
    )
    pick_cols = (part_cols[:, None] == jnp.arange(col_span, dtype=jnp.int32)[None, :]).astype(
        jnp.float32
    )
    return block_sums(pick_cols, mirror, owners)


def body(tiles, coords, counts, valid, start, rotations):
    row_count = lax.axis_size("row")
    col_count = lax.axis_size("col")
    row_index = lax.axis_index("row")
    col_index = lax.axis_index("col")
    slot_count = tiles.shape[2]
    tile_side = tiles.shape[3]
    stretch_nodes = valid.shape[0]
    per_stretch = stretch_nodes // tile_side
    row_span = col_count * per_stretch
    col_span = row_count * per_stretch
    node_total = jnp.float32(stretch_nodes * row_count * col_count)
    vec_count = start.shape[0]
    flat_tiles = tiles.reshape(slot_count, tile_side, tile_side)
    block_rows = coords[0, 0, 0]
    block_cols = coords[0, 0, 1]
    live_count = counts[0, 0]
    global_rows = row_index * row_span + block_rows
    global_cols = (
        block_cols // per_stretch * col_count + col_index
    ) * per_stretch + block_cols % per_stretch
    live = (jnp.arange(slot_count, dtype=jnp.int32) < live_count).astype(jnp.float32)
    mirror_weight = live * (global_rows != global_cols).astype(jnp.float32)

    def graph_product(vectors):
        width = vectors.shape[0]
        short = vectors.astype(jnp.bfloat16)
        col_side = gather_by_exchange(short, "row")
        col_blocks = col_side.reshape(width, col_span, tile_side)
        rows_total = direct_terms(
            flat_tiles, block_rows, block_cols, live, col_blocks, row_span, col_count
        )
        row_side = gather_by_exchange(short, "col")
        rows_total, row_side = lax.optimization_barrier((rows_total, row_side))
        row_blocks = row_side.reshape(width, row_span, tile_side)
        cols_total = mirror_terms(
            flat_tiles, block_rows, block_cols, mirror_weight, row_blocks, col_span, row_count
        )
        direct_part = scatter_sum_by_exchange(rows_total, "col")
        direct_part, cols_total = lax.optimization_barrier((direct_part, cols_total))
        mirror_part = scatter_sum_by_exchange(cols_total, "row")
        return direct_part + mirror_part

    node_mask = valid.astype(jnp.float32)
    first_vecs = start * node_mask[None, :]
    raw = graph_product(jnp.concatenate([node_mask[None, :], first_vecs], 0))
    degree = raw[0]
    first_images = node_mask[None, :] * (degree[None, :] * first_vecs - raw[1:])
    zero_steps = jnp.zeros_like(first_vecs)
    gram_x, gram_ax = gram_sums(first_vecs, first_images)
    vecs, images, steps, step_images, theta = settle(
        first_vecs, first_images, zero_steps, zero_steps, gram_x, gram_ax, node_total
    )
    for turn in range(rotations.shape[0]):
        resid = images - matmul_high(theta, vecs)
        resid_images = node_mask[None, :] * (degree[None, :] * resid - graph_product(resid))
        stacked = jnp.concatenate([vecs, resid, steps], 0)
        stacked_images = jnp.concatenate([images, resid_images, step_images], 0)
        rotation = rotations[turn]
        new_vecs = matmul_high(rotation, stacked)
        new_images = matmul_high(rotation, stacked_images)
        gram_x, gram_ax = gram_sums(new_vecs, new_images)
        new_steps = matmul_high(rotation[:, vec_count:], stacked[vec_count:])
        new_step_images = matmul_high(rotation[:, vec_count:], stacked_images[vec_count:])
        vecs, images, steps, step_images, theta = settle(
            new_vecs, new_images, new_steps, new_step_images, gram_x, gram_ax, node_total
        )
    return (vecs, theta)


def solution(mesh):
    in_specs = (
        P("row", "col", None, None, None),
        P("row", "col", None, None),
        P("row", "col"),
        P(("row", "col")),
        P(None, ("row", "col")),
        P(),
    )
    out_specs = (P(None, ("row", "col")), P())
    return jax.shard_map(body, mesh=mesh, in_specs=in_specs, out_specs=out_specs, check_vma=False)
```

```python
import jax
import jax.numpy as jnp
from jax import lax
from jax.sharding import PartitionSpec as P


def matmul_high(left, right):
    return jnp.dot(left, right, precision=lax.Precision.HIGHEST)


def lower_inverse(lower_factor):
    order_size = lower_factor.shape[0]
    assert order_size <= 8
    identity = jnp.eye(order_size, dtype=lower_factor.dtype)
    diagonal = jnp.diagonal(lower_factor)
    strict = lower_factor / diagonal[:, None] - identity
    square = matmul_high(strict, strict)
    fourth = matmul_high(square, square)
    inverse = matmul_high(matmul_high(identity - strict, identity + square), identity + fourth)
    return inverse / diagonal[None, :]


def settle(new_vecs, new_images, new_steps, step_images, gram_x, gram_ax, node_total):
    lower_factor = jnp.linalg.cholesky(gram_x / node_total, symmetrize_input=False)
    inverse = lower_inverse(lower_factor)
    theta = matmul_high(matmul_high(inverse, gram_ax / node_total), inverse.T)
    return (
        matmul_high(inverse, new_vecs),
        matmul_high(inverse, new_images),
        matmul_high(inverse, new_steps),
        matmul_high(inverse, step_images),
        theta,
    )


def dense_rows(chunks):
    peers, rows, nodes = chunks.shape
    if rows % 8 == 0:
        return chunks
    return chunks.reshape(peers, rows * nodes // 128, 128)


def gather_by_exchange(local, axis):
    count = lax.axis_size(axis)
    copies = jnp.broadcast_to(local[None], (count,) + local.shape)
    held = lax.all_to_all(dense_rows(copies), axis, 0, 0, tiled=True).reshape(copies.shape)
    return jnp.swapaxes(held, 0, 1).reshape(local.shape[0], count * local.shape[1])


def scatter_sum_by_exchange(chunks, axis):
    held = lax.all_to_all(dense_rows(chunks), axis, 0, 0, tiled=True)
    return jnp.sum(held, axis=0).reshape(chunks.shape[1:])


def gram_sums(new_vecs, new_images):
    order = new_vecs.shape[0]
    local = jnp.concatenate(
        [matmul_high(new_vecs, new_vecs.T).reshape(-1), matmul_high(new_images, new_vecs.T).reshape(-1)]
    )
    count = lax.axis_size("row") * lax.axis_size("col")
    copies = jnp.broadcast_to(local[None], (count,) + local.shape)
    held = lax.all_to_all(copies, ("row", "col"), 0, 0, tiled=True)
    total = jnp.sum(held, axis=0)
    return total[: order * order].reshape(order, order), total[order * order :].reshape(order, order)


def block_sums(pick, part_values, owners):
    slots, span = pick.shape
    sums = jnp.einsum(
        "sjb,csu->jcbu",
        pick.reshape(slots, owners, span // owners),
        part_values,
        precision=lax.Precision.HIGHEST,
    )
    return sums.reshape(owners, part_values.shape[0], -1)


def direct_terms(part_tiles, part_rows, part_cols, weight_direct, col_blocks, row_span, owners):
    col_values = jnp.take(col_blocks, part_cols, axis=1)
    direct = (
        jnp.einsum("sut,cst->csu", part_tiles, col_values, preferred_element_type=jnp.float32)
        * weight_direct[None, :, None]
    )
    pick_rows = (part_rows[:, None] == jnp.arange(row_span, dtype=jnp.int32)[None, :]).astype(
        jnp.float32
    )
    return block_sums(pick_rows, direct, owners)


def mirror_terms(part_tiles, part_rows, part_cols, weight_mirror, row_blocks, col_span, owners):
    row_values = jnp.take(row_blocks, part_rows, axis=1)
    mirror = (
        jnp.einsum("sut,csu->cst", part_tiles, row_values, preferred_element_type=jnp.float32)
        * weight_mirror[None, :, None]
    )
    pick_cols = (part_cols[:, None] == jnp.arange(col_span, dtype=jnp.int32)[None, :]).astype(
        jnp.float32
    )
    return block_sums(pick_cols, mirror, owners)


def body(tiles, coords, counts, valid, start, rotations):
    row_count = lax.axis_size("row")
    col_count = lax.axis_size("col")
    row_index = lax.axis_index("row")
    col_index = lax.axis_index("col")
    slot_count = tiles.shape[2]
    tile_side = tiles.shape[3]
    stretch_nodes = valid.shape[0]
    per_stretch = stretch_nodes // tile_side
    row_span = col_count * per_stretch
    col_span = row_count * per_stretch
    node_total = jnp.float32(stretch_nodes * row_count * col_count)
    vec_count = start.shape[0]
    flat_tiles = tiles.reshape(slot_count, tile_side, tile_side)
    block_rows = coords[0, 0, 0]
    block_cols = coords[0, 0, 1]
    live_count = counts[0, 0]
    global_rows = row_index * row_span + block_rows
    global_cols = (
        block_cols // per_stretch * col_count + col_index
    ) * per_stretch + block_cols % per_stretch
    live = (jnp.arange(slot_count, dtype=jnp.int32) < live_count).astype(jnp.float32)
    mirror_weight = live * (global_rows != global_cols).astype(jnp.float32)

    def graph_product(vectors):
        width = vectors.shape[0]
        short = vectors.astype(jnp.bfloat16)
        col_side = gather_by_exchange(short, "row")
        col_blocks = col_side.reshape(width, col_span, tile_side)
        rows_total = direct_terms(
            flat_tiles, block_rows, block_cols, live, col_blocks, row_span, col_count
        )
        row_side = gather_by_exchange(short, "col")
        rows_total, row_side = lax.optimization_barrier((rows_total, row_side))
        row_blocks = row_side.reshape(width, row_span, tile_side)
        cols_total = mirror_terms(
            flat_tiles, block_rows, block_cols, mirror_weight, row_blocks, col_span, row_count
        )
        direct_part = scatter_sum_by_exchange(rows_total, "col")
        direct_part, cols_total = lax.optimization_barrier((direct_part, cols_total))
        mirror_part = scatter_sum_by_exchange(cols_total, "row")
        return direct_part + mirror_part

    node_mask = valid.astype(jnp.float32)
    first_vecs = start * node_mask[None, :]
    raw = graph_product(jnp.concatenate([node_mask[None, :], first_vecs], 0))
    degree = raw[0]
    first_images = node_mask[None, :] * (degree[None, :] * first_vecs - raw[1:])
    zero_steps = jnp.zeros_like(first_vecs)
    gram_x, gram_ax = gram_sums(first_vecs, first_images)
    vecs, images, steps, step_images, theta = settle(
        first_vecs, first_images, zero_steps, zero_steps, gram_x, gram_ax, node_total
    )
    for turn in range(rotations.shape[0]):
        resid = images - matmul_high(theta, vecs)
        resid_images = node_mask[None, :] * (degree[None, :] * resid - graph_product(resid))
        stacked = jnp.concatenate([vecs, resid, steps], 0)
        stacked_images = jnp.concatenate([images, resid_images, step_images], 0)
        rotation = rotations[turn]
        new_vecs = matmul_high(rotation, stacked)
        new_images = matmul_high(rotation, stacked_images)
        gram_x, gram_ax = gram_sums(new_vecs, new_images)
        new_steps = matmul_high(rotation[:, vec_count:], stacked[vec_count:])
        new_step_images = matmul_high(rotation[:, vec_count:], stacked_images[vec_count:])
        vecs, images, steps, step_images, theta = settle(
            new_vecs, new_images, new_steps, new_step_images, gram_x, gram_ax, node_total
        )
    return (vecs, theta)


def solution(mesh):
    in_specs = (
        P("row", "col", None, None, None),
        P("row", "col", None, None),
        P("row", "col"),
        P(("row", "col")),
        P(None, ("row", "col")),
        P(),
    )
    out_specs = (P(None, ("row", "col")), P())
    return jax.shard_map(body, mesh=mesh, in_specs=in_specs, out_specs=out_specs, check_vma=False)
```
